128 devices in a mesh: sub: 8 (over z, core), rng: 16 (over y, x).
Axes of the slice: x: 4, y: 4, z: 4, core: 2. Of those that a mesh axis runs over, the one named last changes fastest.
Arguments:
- echoes: bfloat16 [2, 4096, 8192], P(None, 'sub', 'rng'), may hold values from -6 to 6
- chirp: bfloat16 [2, 512], replicated, may hold values from -0.1875 to 0.1875
- offsets: int32 [3, 8, 2, 512], P(None, 'sub'), may hold values from 0 to 504
- weights: bfloat16 [3, 8, 2, 2, 512, 8], P(None, 'sub'), may hold values from -1 to 1
- owners: int32 [8, 16, 512, 1], P('sub', 'rng'), may hold values from 0 to 127; in each aligned block of 512 rows (0 to 511, 512 to 1023, ..., all dimensions but the last counted through in order) at most 8 rows name the same one
- targets: int32 [8, 16, 512], P('sub', 'rng'), may hold values from 0 to 511
Outputs:
- tiles: bfloat16 [2, 4096, 8192], P(None, 'sub', 'rng')
The draws below stay inside these ranges and needn't reach their ends.
Inputs may be any that keep to these rules, and one draw needn't show every extreme that they name: `owners`: within the 512 rows of one device, no tile is named more than 8 times, a bound that some block reaches.
All inputs are finite; a program needn't handle non-finite values.
Results may differ from the reference program's by a relative error of at most 0.0069.
Values may be sent and summed in bfloat16 or wider, within the bound.
No kernel may reach another device: no remote copies, remote signals or barrier semaphores. Data moves between devices by JAX's collectives and lax.ppermute only.
A program may use at most 384 MiB of HBM per device.

```python
import math
import jax
import jax.numpy as jnp
import numpy as np
from jax import lax

P_DEV = 512
R_DEV = 512
CHIRP = 512
RBLK = 512
TAPS = 8
SECTIONS = 3
SUBS = 8
BLOCKS = 16
PULSES = 4096
RANGE = 8192
TILE_ROWS = 512
CAP = 8
DEVICES = 128


def touch_ends(drawn, stream_key, smallest, high):
    shape = drawn.shape
    spot = [jax.random.randint(jax.random.fold_in(stream_key, axis), (), 0, shape[axis]) for axis in range(len(shape))]
    drawn = drawn.at[tuple(spot)].set(smallest)
    longest = shape.index(max(shape))
    spot[longest] = (spot[longest] + 1) % shape[longest]
    return drawn.at[tuple(spot)].set(high)


def block_levels(own_key, dims, split, least, largest):
    def one(position, blocks):
        draws = jax.random.uniform(jax.random.fold_in(jax.random.fold_in(own_key, 6), position), (blocks,), jnp.float32, least / len(split), largest / len(split))
        return jnp.repeat(jnp.exp(draws), dims[position] // blocks).reshape((-1,) + (1,) * (len(dims) - position - 1))

    gain = one(*split[0])
    for cut in split[1:]:
        gain = gain * one(*cut)
    return gain


def shared_out(stream_key, own, number, rows, number_of, top, reach, slope):
    order = jax.random.permutation(stream_key, number_of)
    heavy_load, usual = portions_of(number_of, rows * top, reach, slope, True), portions_of(number_of, rows * top, reach, slope, False)
    places = jnp.arange(number_of)

    def named(tallies, offset_by):
        used = int((tallies > 0).sum())
        fixed = max(1, used // 4)
        moved = fixed + (places - fixed + offset_by * (used - fixed)) % max(1, number_of - fixed)
        return jnp.zeros((number_of,), jnp.int32).at[order[jnp.where(places < fixed, places, moved)]].set(jnp.asarray(tallies, jnp.int32))

    tallies = jnp.where(number % 4 == 0, named(heavy_load, number // 4), named(usual, number - number // 4 - 1))
    mixed = jax.random.permutation(jax.random.fold_in(own, 3), number_of)
    source_of, sink = mixed[0:number_of // 2 * 2:2], mixed[1:number_of // 2 * 2:2]
    slack = jnp.minimum(tallies[source_of] - 1, reach - tallies[sink]) // 2
    slack = jnp.where((source_of == order[0]) | (sink == order[0]) | (tallies[sink] == 0), 0, jnp.maximum(slack, 0))
    moved = jax.random.randint(jax.random.fold_in(own, 4), (number_of // 2,), 0, 1 << 20) % (slack + 1)
    tallies = tallies.at[source_of].add(-moved).at[sink].add(moved)
    members = jnp.searchsorted(jnp.cumsum(tallies), jnp.arange(rows * top), side="right").astype(jnp.int32)
    table = members.reshape(top, rows).T
    table = table[jax.random.permutation(jax.random.fold_in(own, 1), rows)]
    offset_by = jax.random.randint(jax.random.fold_in(own, 2), (rows, 1), 0, top)
    return jnp.take_along_axis(table, (jnp.arange(top)[None, :] + offset_by) % top, axis=1)


def portions_of(number_of, total, bound, lean, full):
    weights = [(1 << 20) // math.isqrt(rank ** lean) + 1 for rank in range(1, number_of + 1)]
    largest = bound if full else min(bound, max(-(-total // number_of), total * weights[0] // sum(weights)))
    least = 1 if total - largest >= number_of - 1 else 0
    given, rest = [largest] + [least] * (number_of - 1), total - largest - least * (number_of - 1)
    while rest > 0:
        candidates = [i for i in range(1, number_of) if given[i] < largest] or [i for i in range(1, number_of) if given[i] < bound]
        whole, remaining = sum([weights[i] for i in candidates]), rest
        for i in candidates:
            addition = min(bound - given[i], max(1, remaining * weights[i] // whole), rest)
            given[i] = given[i] + addition
            rest = rest - addition
    return np.array(given)


def scatter_about(key, dims, scale, most, cuts=(), kind=jnp.bfloat16):
    level = block_levels(key, dims, cuts, -0.22, 0.18) if cuts else 1.0
    array = jax.random.normal(key, dims, jnp.float32) * scale * level
    return jnp.minimum(jnp.maximum(array, -most), most).astype(kind)


def setup_inputs(seed: int = 0) -> dict:
    key_list = jax.random.split(jax.random.key(seed), 7)
    echoes = scatter_about(key_list[0], (2, PULSES, RANGE), 1.0, 6.0, ((1, 8), (2, 16)))
    chirp = scatter_about(key_list[1], (2, CHIRP), (2 * CHIRP) ** -0.5, 0.1875)
    offsets = touch_ends(jax.random.randint(key_list[2], (SECTIONS, SUBS, 2, P_DEV), 0, P_DEV - TAPS + 1), jax.random.fold_in(key_list[2], 1), 0, P_DEV - TAPS).astype(jnp.int32)
    weights = scatter_about(key_list[3], (SECTIONS, SUBS, 2, 2, P_DEV, TAPS), (4 * TAPS) ** -0.5, 1.0, ((1, 8),))
    owners_keys = jax.random.split(jax.random.fold_in(key_list[4], 1), SUBS * BLOCKS * P_DEV // P_DEV)
    owners_turns = jax.random.permutation(jax.random.fold_in(key_list[4], 3), SUBS * BLOCKS * P_DEV // P_DEV)
    owners = jax.vmap(lambda own, number: shared_out(jax.random.fold_in(key_list[4], 2), own, number, P_DEV, DEVICES, 1, CAP, 2))(owners_keys, owners_turns).reshape((SUBS, BLOCKS, P_DEV, 1))
    targets = touch_ends(jax.random.randint(key_list[5], (SUBS, BLOCKS, P_DEV), 0, TILE_ROWS), jax.random.fold_in(key_list[5], 1), 0, TILE_ROWS - 1).astype(jnp.int32)
    return {"echoes": echoes, "chirp": chirp, "offsets": offsets, "weights": weights, "owners": owners, "targets": targets}


def replica_matrix(chirp, block_len):
    taps_len = chirp.shape[1]
    width = block_len + taps_len
    parts = []
    for part in range(2):
        padded = jnp.concatenate([chirp[part], jnp.zeros((width + 1 - taps_len,), chirp.dtype)])
        tiled = jnp.tile(padded, block_len)[: block_len * width].reshape(block_len, width)
        parts.append(tiled.T)
    h_real, h_imag = parts[0], parts[1]
    upper = jnp.concatenate([h_real, -h_imag], axis=1)
    lower = jnp.concatenate([h_imag, h_real], axis=1)
    return jnp.concatenate([upper, lower], axis=0)


def reference(echoes, chirp, offsets, weights, owners, targets):
    matrix = replica_matrix(chirp, RBLK)
    padded = jnp.pad(echoes, ((0, 0), (0, 0), (0, CHIRP)))

    def compress(index):
        window = lax.dynamic_slice_in_dim(padded, index * RBLK, RBLK + CHIRP, 2)
        stacked = jnp.concatenate([window[0], window[1]], axis=1)
        return jnp.dot(stacked, matrix, preferred_element_type=jnp.float32).astype(jnp.bfloat16)

    count_blocks = RANGE // RBLK
    pieces = lax.map(compress, jnp.arange(count_blocks, dtype=jnp.int32))
    compressed = pieces.reshape(count_blocks, PULSES, 2, RBLK).transpose(2, 1, 0, 3).reshape(2, PULSES, RANGE)
    image = compressed.reshape(2, SUBS, P_DEV, RANGE).transpose(1, 0, 2, 3)
    for section in range(SECTIONS):
        order = np.arange(SUBS) ^ (1 << section)
        sources = (image, image[order])
        real_acc = jnp.zeros((SUBS, P_DEV, RANGE), jnp.float32)
        imag_acc = jnp.zeros((SUBS, P_DEV, RANGE), jnp.float32)
        for side in range(2):
            for tap in range(TAPS):
                index = (offsets[section, :, side, :] + tap).astype(jnp.int32)
                taken = jnp.take_along_axis(sources[side], index[:, None, :, None], axis=2).astype(jnp.float32)
                w_real = weights[section, :, side, 0, :, tap].astype(jnp.float32)[:, :, None]
                w_imag = weights[section, :, side, 1, :, tap].astype(jnp.float32)[:, :, None]
                real_acc = real_acc + w_real * taken[:, 0] - w_imag * taken[:, 1]
                imag_acc = imag_acc + w_real * taken[:, 1] + w_imag * taken[:, 0]
        image = jnp.stack([real_acc, imag_acc], axis=1).astype(jnp.bfloat16)
    rows = image.reshape(SUBS, 2, P_DEV, BLOCKS, R_DEV).transpose(0, 3, 2, 1, 4).reshape(SUBS * BLOCKS * P_DEV, 2, R_DEV)
    flat_index = (owners.reshape(-1) * TILE_ROWS + targets.reshape(-1)).astype(jnp.int32)
    summed = jnp.zeros((DEVICES * TILE_ROWS, 2, R_DEV), jnp.float32).at[flat_index].add(rows.astype(jnp.float32))
    result = summed.reshape(SUBS, BLOCKS, TILE_ROWS, 2, R_DEV).transpose(3, 0, 2, 1, 4)
    return result.reshape(2, SUBS * TILE_ROWS, RANGE).astype(jnp.bfloat16)
```

```python
import jax
import jax.numpy as jnp
from jax import lax
from jax.sharding import PartitionSpec as P

RBLK = 512


def shifted(value, axis, steps):
    count = lax.axis_size(axis)
    first, last = (max(0, -steps), min(count, count - steps))
    return lax.ppermute(value, axis, [(source, source + steps) for source in range(first, last)])


def from_partner(value, axis, apart):
    return lax.ppermute(value, axis, [(i, i ^ 1 << apart) for i in range(lax.axis_size(axis))])


def replica_matrix(chirp, block_len):
    taps_len = chirp.shape[1]
    width = block_len + taps_len
    parts = []
    for part in range(2):
        padded = jnp.concatenate([chirp[part], jnp.zeros((width + 1 - taps_len,), chirp.dtype)])
        tiled = jnp.tile(padded, block_len)[: block_len * width].reshape(block_len, width)
        parts.append(tiled.T)
    h_real, h_imag = (parts[0], parts[1])
    upper = jnp.concatenate([h_real, -h_imag], axis=1)
    lower = jnp.concatenate([h_imag, h_real], axis=1)
    return jnp.concatenate([upper, lower], axis=0)


def merge_matrix(starts, kernel):
    beams = starts.shape[0]
    taps_len = kernel.shape[-1]
    shift = jnp.arange(beams, dtype=jnp.int32)[None, :] - starts[:, None]
    g_real = jnp.zeros((beams, beams), kernel.dtype)
    g_imag = jnp.zeros((beams, beams), kernel.dtype)
    for tap in range(taps_len):
        hit = shift == tap
        g_real = jnp.where(hit, kernel[0][:, tap : tap + 1], g_real)
        g_imag = jnp.where(hit, kernel[1][:, tap : tap + 1], g_imag)
    upper = jnp.concatenate([g_real, -g_imag], axis=1)
    lower = jnp.concatenate([g_imag, g_real], axis=1)
    return jnp.concatenate([upper, lower], axis=0)


def group_slots(dest, devices):
    onehot = (dest[:, None] == jnp.arange(devices, dtype=jnp.int32)[None, :]).astype(jnp.int32)
    return jnp.sum((jnp.cumsum(onehot, axis=0) - 1) * onehot, axis=1)


def route_rows(send, labels):
    got = lax.all_to_all(send, ("sub", "rng"), split_axis=0, concat_axis=0, tiled=True)
    table = lax.all_gather(labels.astype(jnp.float32), ("sub", "rng"), axis=0)
    me = lax.axis_index("sub") * lax.axis_size("rng") + lax.axis_index("rng")
    marks = lax.dynamic_index_in_dim(table, me, axis=1, keepdims=False).astype(jnp.int32)
    return (got, marks)


def on_device(echoes, chirp, offsets, weights, owners, targets):
    p_dev = echoes.shape[1]
    r_dev = echoes.shape[2]
    n_sub = lax.axis_size("sub")
    n_rng = lax.axis_size("rng")
    devices = n_sub * n_rng
    capacity = max(2, 2 * p_dev // devices)
    tail = shifted(echoes, "rng", -1)
    extended = jnp.concatenate([echoes, tail], axis=2)
    matrix = replica_matrix(chirp, RBLK)
    stacked = jnp.concatenate([extended[0], extended[1]], axis=1)
    block_out = jnp.dot(stacked, matrix, preferred_element_type=jnp.float32).astype(jnp.bfloat16)
    pieces = block_out.reshape(p_dev, 2, RBLK)
    image = pieces.transpose(1, 0, 2).reshape(2 * p_dev, r_dev)
    section_count = offsets.shape[0]
    for section in range(section_count):
        partner = from_partner(image, "sub", section)
        mine = merge_matrix(offsets[section, 0, 0], weights[section, 0, 0])
        theirs = merge_matrix(offsets[section, 0, 1], weights[section, 0, 1])
        merged = jnp.dot(mine, image, preferred_element_type=jnp.float32)
        merged = merged + jnp.dot(theirs, partner, preferred_element_type=jnp.float32)
        image = merged.astype(jnp.bfloat16)
    rows = image.reshape(2, p_dev, r_dev).transpose(1, 0, 2).reshape(p_dev, 2 * r_dev)
    dest = owners.reshape(p_dev)
    aim = targets.reshape(p_dev)
    slot = dest * capacity + group_slots(dest, devices)
    pick = jnp.arange(devices * capacity, dtype=jnp.int32)[:, None] == slot[None, :]
    send = jnp.dot(pick.astype(jnp.bfloat16), rows, preferred_element_type=jnp.float32).astype(
        jnp.bfloat16
    )
    labels = jnp.sum(jnp.where(pick, aim[None, :] + 1, 0), axis=1) - 1
    got, marks = route_rows(
        send.reshape(devices, capacity, 2 * r_dev), labels.reshape(devices, capacity)
    )
    got_flat = got.reshape(devices * capacity, 2 * r_dev)
    mark_flat = marks.reshape(devices * capacity)
    place = (jnp.arange(p_dev, dtype=jnp.int32)[:, None] == mark_flat[None, :]).astype(jnp.bfloat16)
    tile = jnp.dot(place, got_flat, preferred_element_type=jnp.float32).astype(jnp.bfloat16)
    return tile.reshape(p_dev, 2, r_dev).transpose(1, 0, 2)


def solution(mesh):
    in_specs = (
        P(None, "sub", "rng"),
        P(),
        P(None, "sub", None, None),
        P(None, "sub", None, None, None, None),
        P("sub", "rng", None, None),
        P("sub", "rng", None),
    )
    out_specs = P(None, "sub", "rng")
    return jax.shard_map(
        on_device, mesh=mesh, in_specs=in_specs, out_specs=out_specs, check_vma=False
    )
```

```python
import jax
import jax.numpy as jnp
from jax import lax
from jax.sharding import PartitionSpec as P

RBLK = 512


def shifted(value, axis, steps):
    count = lax.axis_size(axis)
    first, last = (max(0, -steps), min(count, count - steps))
    return lax.ppermute(value, axis, [(source, source + steps) for source in range(first, last)])


def from_partner(value, axis, apart):
    return lax.ppermute(value, axis, [(i, i ^ 1 << apart) for i in range(lax.axis_size(axis))])


def replica_matrix(chirp, block_len):
    taps_len = chirp.shape[1]
    width = block_len + taps_len
    parts = []
    for part in range(2):
        padded = jnp.concatenate([chirp[part], jnp.zeros((width + 1 - taps_len,), chirp.dtype)])
        tiled = jnp.tile(padded, block_len)[: block_len * width].reshape(block_len, width)
        parts.append(tiled.T)
    h_real, h_imag = (parts[0], parts[1])
    upper = jnp.concatenate([h_real, -h_imag], axis=1)
    lower = jnp.concatenate([h_imag, h_real], axis=1)
    return jnp.concatenate([upper, lower], axis=0)


def merge_matrix(starts, kernel):
    beams = starts.shape[0]
    taps_len = kernel.shape[-1]
    shift = jnp.arange(beams, dtype=jnp.int32)[None, :] - starts[:, None]
    g_real = jnp.zeros((beams, beams), kernel.dtype)
    g_imag = jnp.zeros((beams, beams), kernel.dtype)
    for tap in range(taps_len):
        hit = shift == tap
        g_real = jnp.where(hit, kernel[0][:, tap : tap + 1], g_real)
        g_imag = jnp.where(hit, kernel[1][:, tap : tap + 1], g_imag)
    upper = jnp.concatenate([g_real, -g_imag], axis=1)
    lower = jnp.concatenate([g_imag, g_real], axis=1)
    return jnp.concatenate([upper, lower], axis=0)


def group_slots(dest, devices):
    onehot = (dest[:, None] == jnp.arange(devices, dtype=jnp.int32)[None, :]).astype(jnp.int32)
    return jnp.sum((jnp.cumsum(onehot, axis=0) - 1) * onehot, axis=1)


def route_rows(send):
    n_sub = lax.axis_size("sub")
    n_rng = lax.axis_size("rng")
    grid = send.reshape((n_sub, n_rng) + send.shape[1:])
    grid = lax.all_to_all(grid, "rng", split_axis=1, concat_axis=1, tiled=True)
    grid = lax.all_to_all(grid, "sub", split_axis=0, concat_axis=0, tiled=True)
    return grid.reshape(send.shape)


def on_device(echoes, chirp, offsets, weights, owners, targets):
    p_dev = echoes.shape[1]
    r_dev = echoes.shape[2]
    n_sub = lax.axis_size("sub")
    n_rng = lax.axis_size("rng")
    devices = n_sub * n_rng
    capacity = max(2, 2 * p_dev // devices)
    tail = shifted(echoes, "rng", -1)
    extended = jnp.concatenate([echoes, tail], axis=2)
    matrix = replica_matrix(chirp, RBLK)
    stacked = jnp.concatenate([extended[0], extended[1]], axis=1)
    block_out = jnp.dot(stacked, matrix, preferred_element_type=jnp.float32).astype(jnp.bfloat16)
    pieces = block_out.reshape(p_dev, 2, RBLK)
    image = pieces.transpose(1, 0, 2).reshape(2 * p_dev, r_dev)
    section_count = offsets.shape[0]
    for section in range(section_count):
        partner = from_partner(image, "sub", section)
        mine = merge_matrix(offsets[section, 0, 0], weights[section, 0, 0])
        theirs = merge_matrix(offsets[section, 0, 1], weights[section, 0, 1])
        merged = jnp.dot(mine, image, preferred_element_type=jnp.float32)
        merged = merged + jnp.dot(theirs, partner, preferred_element_type=jnp.float32)
        image = merged.astype(jnp.bfloat16)
    rows = image.reshape(2, p_dev, r_dev).transpose(1, 0, 2).reshape(p_dev, 2 * r_dev)
    dest = owners.reshape(p_dev)
    aim = targets.reshape(p_dev)
    slot = dest * capacity + group_slots(dest, devices)
    pick = jnp.arange(devices * capacity, dtype=jnp.int32)[:, None] == slot[None, :]
    code = aim + 1
    lanes = jnp.arange(128, dtype=jnp.int32)[None, :]
    extra = jnp.where(lanes == 0, (code // 32)[:, None], jnp.where(lanes == 1, (code % 32)[:, None], 0))
    rows = jnp.concatenate([rows, extra.astype(jnp.bfloat16)], axis=1)
    send = jnp.dot(pick.astype(jnp.bfloat16), rows, preferred_element_type=jnp.float32).astype(
        jnp.bfloat16
    )
    width = 2 * r_dev
    got = route_rows(send.reshape(devices, capacity, width + 128))
    got_flat = got.reshape(devices * capacity, width + 128)
    head = got_flat[:, width].astype(jnp.int32)
    low = got_flat[:, width + 1].astype(jnp.int32)
    mark_flat = head * 32 + low - 1
    place = (jnp.arange(p_dev, dtype=jnp.int32)[:, None] == mark_flat[None, :]).astype(jnp.bfloat16)
    tile = jnp.dot(place, got_flat[:, :width], preferred_element_type=jnp.float32).astype(jnp.bfloat16)
    return tile.reshape(p_dev, 2, r_dev).transpose(1, 0, 2)


def solution(mesh):
    in_specs = (
        P(None, "sub", "rng"),
        P(),
        P(None, "sub", None, None),
        P(None, "sub", None, None, None, None),
        P("sub", "rng", None, None),
        P("sub", "rng", None),
    )
    out_specs = P(None, "sub", "rng")
    return jax.shard_map(
        on_device, mesh=mesh, in_specs=in_specs, out_specs=out_specs, check_vma=False
    )
```

```python
import jax
import jax.numpy as jnp
from jax import lax
from jax.sharding import PartitionSpec as P

RBLK = 512


def shifted(value, axis, steps):
    count = lax.axis_size(axis)
    first, last = (max(0, -steps), min(count, count - steps))
    return lax.ppermute(value, axis, [(source, source + steps) for source in range(first, last)])


def from_partner(value, axis, apart):
    return lax.ppermute(value, axis, [(i, i ^ 1 << apart) for i in range(lax.axis_size(axis))])


def replica_matrix(chirp, block_len):
    taps_len = chirp.shape[1]
    width = block_len + taps_len
    parts = []
    for part in range(2):
        padded = jnp.concatenate([chirp[part], jnp.zeros((width + 1 - taps_len,), chirp.dtype)])
        tiled = jnp.tile(padded, block_len)[: block_len * width].reshape(block_len, width)
        parts.append(tiled.T)
    h_real, h_imag = (parts[0], parts[1])
    upper = jnp.concatenate([h_real, -h_imag], axis=1)
    lower = jnp.concatenate([h_imag, h_real], axis=1)
    return jnp.concatenate([upper, lower], axis=0)


def merge_matrix(starts, kernel):
    beams = starts.shape[0]
    taps_len = kernel.shape[-1]
    shift = jnp.arange(beams, dtype=jnp.int32)[None, :] - starts[:, None]
    g_real = jnp.zeros((beams, beams), kernel.dtype)
    g_imag = jnp.zeros((beams, beams), kernel.dtype)
    for tap in range(taps_len):
        hit = shift == tap
        g_real = jnp.where(hit, kernel[0][:, tap : tap + 1], g_real)
        g_imag = jnp.where(hit, kernel[1][:, tap : tap + 1], g_imag)
    upper = jnp.concatenate([g_real, -g_imag], axis=1)
    lower = jnp.concatenate([g_imag, g_real], axis=1)
    return jnp.concatenate([upper, lower], axis=0)


def group_slots(dest, devices):
    onehot = (dest[:, None] == jnp.arange(devices, dtype=jnp.int32)[None, :]).astype(jnp.int32)
    return jnp.sum((jnp.cumsum(onehot, axis=0) - 1) * onehot, axis=1)


def route_rows(send):
    return lax.all_to_all(send, ("sub", "rng"), split_axis=0, concat_axis=0, tiled=True)


def on_device(echoes, chirp, offsets, weights, owners, targets):
    p_dev = echoes.shape[1]
    r_dev = echoes.shape[2]
    n_sub = lax.axis_size("sub")
    n_rng = lax.axis_size("rng")
    devices = n_sub * n_rng
    capacity = max(2, 2 * p_dev // devices)
    tail = shifted(echoes, "rng", -1)
    extended = jnp.concatenate([echoes, tail], axis=2)
    matrix = replica_matrix(chirp, RBLK)
    stacked = jnp.concatenate([extended[0], extended[1]], axis=1)
    block_out = jnp.dot(stacked, matrix, preferred_element_type=jnp.float32).astype(jnp.bfloat16)
    pieces = block_out.reshape(p_dev, 2, RBLK)
    image = pieces.transpose(1, 0, 2).reshape(2 * p_dev, r_dev)
    section_count = offsets.shape[0]
    for section in range(section_count):
        partner = from_partner(image, "sub", section)
        mine = merge_matrix(offsets[section, 0, 0], weights[section, 0, 0])
        theirs = merge_matrix(offsets[section, 0, 1], weights[section, 0, 1])
        merged = jnp.dot(mine, image, preferred_element_type=jnp.float32)
        merged = merged + jnp.dot(theirs, partner, preferred_element_type=jnp.float32)
        image = merged.astype(jnp.bfloat16)
    rows = image.reshape(2, p_dev, r_dev).transpose(1, 0, 2).reshape(p_dev, 2 * r_dev)
    dest = owners.reshape(p_dev)
    aim = targets.reshape(p_dev)
    slot = dest * capacity + group_slots(dest, devices)
    pick = jnp.arange(devices * capacity, dtype=jnp.int32)[:, None] == slot[None, :]
    code = aim + 1
    lanes = jnp.arange(128, dtype=jnp.int32)[None, :]
    extra = jnp.where(lanes == 0, (code // 32)[:, None], jnp.where(lanes == 1, (code % 32)[:, None], 0))
    rows = jnp.concatenate([rows, extra.astype(jnp.bfloat16)], axis=1)
    send = jnp.dot(pick.astype(jnp.bfloat16), rows, preferred_element_type=jnp.float32).astype(
        jnp.bfloat16
    )
    width = 2 * r_dev
    got = route_rows(send.reshape(devices, capacity, width + 128))
    got_flat = got.reshape(devices * capacity, width + 128)
    head = got_flat[:, width].astype(jnp.int32)
    low = got_flat[:, width + 1].astype(jnp.int32)
    mark_flat = head * 32 + low - 1
    place = (jnp.arange(p_dev, dtype=jnp.int32)[:, None] == mark_flat[None, :]).astype(jnp.bfloat16)
    tile = jnp.dot(place, got_flat[:, :width], preferred_element_type=jnp.float32).astype(jnp.bfloat16)
    return tile.reshape(p_dev, 2, r_dev).transpose(1, 0, 2)


def solution(mesh):
    in_specs = (
        P(None, "sub", "rng"),
        P(),
        P(None, "sub", None, None),
        P(None, "sub", None, None, None, None),
        P("sub", "rng", None, None),
        P("sub", "rng", None),
    )
    out_specs = P(None, "sub", "rng")
    return jax.shard_map(
        on_device, mesh=mesh, in_specs=in_specs, out_specs=out_specs, check_vma=False
    )
```

```python
import jax
import jax.numpy as jnp
from jax import lax
from jax.sharding import PartitionSpec as P

RBLK = 512


def shifted(value, axis, steps):
    count = lax.axis_size(axis)
    first, last = (max(0, -steps), min(count, count - steps))
    return lax.ppermute(value, axis, [(source, source + steps) for source in range(first, last)])


def from_partner(value, axis, apart):
    return lax.ppermute(value, axis, [(i, i ^ 1 << apart) for i in range(lax.axis_size(axis))])


def replica_matrix(chirp, block_len):
    taps_len = chirp.shape[1]
    width = block_len + taps_len
    parts = []
    for part in range(2):
        padded = jnp.concatenate([chirp[part], jnp.zeros((width + 1 - taps_len,), chirp.dtype)])
        tiled = jnp.tile(padded, block_len)[: block_len * width].reshape(block_len, width)
        parts.append(tiled.T)
    h_real, h_imag = (parts[0], parts[1])
    upper = jnp.concatenate([h_real, -h_imag], axis=1)
    lower = jnp.concatenate([h_imag, h_real], axis=1)
    return jnp.concatenate([upper, lower], axis=0)


def merge_matrix(starts, kernel):
    beams = starts.shape[0]
    taps_len = kernel.shape[-1]
    shift = jnp.arange(beams, dtype=jnp.int32)[None, :] - starts[:, None]
    g_real = jnp.zeros((beams, beams), kernel.dtype)
    g_imag = jnp.zeros((beams, beams), kernel.dtype)
    for tap in range(taps_len):
        hit = shift == tap
        g_real = jnp.where(hit, kernel[0][:, tap : tap + 1], g_real)
        g_imag = jnp.where(hit, kernel[1][:, tap : tap + 1], g_imag)
    upper = jnp.concatenate([g_real, -g_imag], axis=1)
    lower = jnp.concatenate([g_imag, g_real], axis=1)
    return jnp.concatenate([upper, lower], axis=0)


def group_slots(dest, devices):
    onehot = (dest[:, None] == jnp.arange(devices, dtype=jnp.int32)[None, :]).astype(jnp.int32)
    return jnp.sum((jnp.cumsum(onehot, axis=0) - 1) * onehot, axis=1)


def route_rows(send):
    return lax.all_to_all(send, ("sub", "rng"), split_axis=0, concat_axis=0, tiled=True)


CHUNKS = 2


def on_device(echoes, chirp, offsets, weights, owners, targets):
    p_dev = echoes.shape[1]
    r_dev = echoes.shape[2]
    n_sub = lax.axis_size("sub")
    n_rng = lax.axis_size("rng")
    devices = n_sub * n_rng
    capacity = max(2, 2 * p_dev // devices)
    width = r_dev // CHUNKS
    tails = [shifted(echoes[:, :, c * width : (c + 1) * width], "rng", -1) for c in range(CHUNKS)]
    matrix = replica_matrix(chirp, width)
    images = []
    for c in range(CHUNKS):
        window = jnp.concatenate([echoes[:, :, c * width :]] + tails[: c + 1], axis=2)
        stacked = jnp.concatenate([window[0], window[1]], axis=1)
        block_out = jnp.dot(stacked, matrix, preferred_element_type=jnp.float32).astype(jnp.bfloat16)
        images.append(block_out.reshape(p_dev, 2, width).transpose(1, 0, 2).reshape(2 * p_dev, width))
    section_count = offsets.shape[0]
    for section in range(section_count):
        mine = merge_matrix(offsets[section, 0, 0], weights[section, 0, 0])
        theirs = merge_matrix(offsets[section, 0, 1], weights[section, 0, 1])
        partners = [from_partner(image, "sub", section) for image in images]
        merged = []
        for image, partner in zip(images, partners):
            acc = jnp.dot(mine, image, preferred_element_type=jnp.float32)
            acc = acc + jnp.dot(theirs, partner, preferred_element_type=jnp.float32)
            merged.append(acc.astype(jnp.bfloat16))
        images = merged
    dest = owners.reshape(p_dev)
    aim = targets.reshape(p_dev)
    slot = dest * capacity + group_slots(dest, devices)
    pick = (jnp.arange(devices * capacity, dtype=jnp.int32)[:, None] == slot[None, :]).astype(
        jnp.bfloat16
    )
    code = aim + 1
    lanes = jnp.arange(128, dtype=jnp.int32)[None, :]
    extra = jnp.where(lanes == 0, (code // 32)[:, None], jnp.where(lanes == 1, (code % 32)[:, None], 0))
    received = []
    for c, image in enumerate(images):
        rows = image.reshape(2, p_dev, width).transpose(1, 0, 2).reshape(p_dev, 2 * width)
        if c == 0:
            rows = jnp.concatenate([rows, extra.astype(jnp.bfloat16)], axis=1)
        send = jnp.dot(pick, rows, preferred_element_type=jnp.float32).astype(jnp.bfloat16)
        got = route_rows(send.reshape(devices, capacity, rows.shape[1]))
        received.append(got.reshape(devices * capacity, rows.shape[1]))
    head = received[0][:, 2 * width].astype(jnp.int32)
    low = received[0][:, 2 * width + 1].astype(jnp.int32)
    mark_flat = head * 32 + low - 1
    place = (jnp.arange(p_dev, dtype=jnp.int32)[:, None] == mark_flat[None, :]).astype(jnp.bfloat16)
    tiles = []
    for got in received:
        tile = jnp.dot(place, got[:, : 2 * width], preferred_element_type=jnp.float32)
        tiles.append(tile.astype(jnp.bfloat16).reshape(p_dev, 2, width))
    return jnp.concatenate(tiles, axis=2).transpose(1, 0, 2)


def solution(mesh):
    in_specs = (
        P(None, "sub", "rng"),
        P(),
        P(None, "sub", None, None),
        P(None, "sub", None, None, None, None),
        P("sub", "rng", None, None),
        P("sub", "rng", None),
    )
    out_specs = P(None, "sub", "rng")
    return jax.shard_map(
        on_device, mesh=mesh, in_specs=in_specs, out_specs=out_specs, check_vma=False
    )
```

```python
import jax
import jax.numpy as jnp
from jax import lax
from jax.sharding import PartitionSpec as P

RBLK = 512


def shifted(value, axis, steps):
    count = lax.axis_size(axis)
    first, last = (max(0, -steps), min(count, count - steps))
    return lax.ppermute(value, axis, [(source, source + steps) for source in range(first, last)])


def from_partner(value, axis, apart):
    return lax.ppermute(value, axis, [(i, i ^ 1 << apart) for i in range(lax.axis_size(axis))])


def replica_matrix(chirp, block_len):
    taps_len = chirp.shape[1]
    width = block_len + taps_len
    parts = []
    for part in range(2):
        padded = jnp.concatenate([chirp[part], jnp.zeros((width + 1 - taps_len,), chirp.dtype)])
        tiled = jnp.tile(padded, block_len)[: block_len * width].reshape(block_len, width)
        parts.append(tiled.T)
    h_real, h_imag = (parts[0], parts[1])
    upper = jnp.concatenate([h_real, -h_imag], axis=1)
    lower = jnp.concatenate([h_imag, h_real], axis=1)
    return jnp.concatenate([upper, lower], axis=0)


def band_parts(starts, kernel):
    beams = starts.shape[0]
    taps_len = kernel.shape[-1]
    shift = jnp.arange(beams, dtype=jnp.int32)[None, :] - starts[:, None]
    g_real = jnp.zeros((beams, beams), kernel.dtype)
    g_imag = jnp.zeros((beams, beams), kernel.dtype)
    for tap in range(taps_len):
        hit = shift == tap
        g_real = jnp.where(hit, kernel[0][:, tap : tap + 1], g_real)
        g_imag = jnp.where(hit, kernel[1][:, tap : tap + 1], g_imag)
    return g_real, g_imag


def apply_band(parts, source):
    g_real, g_imag = parts
    beams = g_real.shape[0]
    s_real, s_imag = source[:beams], source[beams:]

    def dot(a, b):
        return jnp.dot(a, b, preferred_element_type=jnp.float32)

    return dot(g_real, s_real) - dot(g_imag, s_imag), dot(g_imag, s_real) + dot(g_real, s_imag)


def group_slots(dest, devices):
    onehot = (dest[:, None] == jnp.arange(devices, dtype=jnp.int32)[None, :]).astype(jnp.int32)
    return jnp.sum((jnp.cumsum(onehot, axis=0) - 1) * onehot, axis=1)


def xor_fetch(value, mask):
    return lax.ppermute(value, "sub", [(i, i ^ mask) for i in range(lax.axis_size("sub"))])


SPLIT = (False, True, True)


def on_device(echoes, chirp, offsets, weights, owners, targets):
    p_dev = echoes.shape[1]
    r_dev = echoes.shape[2]
    n_sub = lax.axis_size("sub")
    n_rng = lax.axis_size("rng")
    devices = n_sub * n_rng
    capacity = max(2, 2 * p_dev // devices)
    section_count = offsets.shape[0]
    me_sub = lax.axis_index("sub")
    masks = [0]
    for section in range(section_count):
        if SPLIT[section]:
            masks = masks + [m ^ (1 << section) for m in masks]
    own = (weights, offsets, owners, targets)
    flat = jnp.concatenate([a.reshape(-1).astype(jnp.float32) for a in own])
    side = {0: own}
    for m in masks[1:]:
        got = xor_fetch(flat, m)
        parts = []
        at = 0
        for a in own:
            parts.append(got[at : at + a.size].reshape(a.shape).astype(a.dtype))
            at += a.size
        side[m] = tuple(parts)
    tail = shifted(echoes, "rng", -1)
    extended = jnp.concatenate([echoes, tail], axis=2)
    matrix = replica_matrix(chirp, RBLK)
    stacked = jnp.concatenate([extended[0], extended[1]], axis=1)
    block_out = jnp.dot(stacked, matrix, preferred_element_type=jnp.float32).astype(jnp.bfloat16)
    image = block_out.reshape(p_dev, 2, RBLK).transpose(1, 0, 2).reshape(2 * p_dev, r_dev)
    pieces = {0: image}
    width = r_dev
    col_start = 0
    for section in range(section_count):
        bit = 1 << section
        if SPLIT[section]:
            half = width // 2
            mine_bit = (me_sub >> section) & 1
            col_start = col_start + mine_bit * half
            old = {}
            for m, piece in pieces.items():
                old[m] = lax.dynamic_slice_in_dim(piece, mine_bit * half, half, axis=1)
                sent = lax.dynamic_slice_in_dim(piece, (1 - mine_bit) * half, half, axis=1)
                old[m ^ bit] = xor_fetch(sent, bit)
            width = half
        else:
            old = dict(pieces)
            for m, piece in pieces.items():
                old[m ^ bit] = xor_fetch(piece, bit)
        keys = sorted(old) if SPLIT[section] else sorted(pieces)
        new = {}
        for m in keys:
            w_m, o_m = side[m][0], side[m][1]
            mine = band_parts(o_m[section, 0, 0], w_m[section, 0, 0])
            theirs = band_parts(o_m[section, 0, 1], w_m[section, 0, 1])
            a_real, a_imag = apply_band(mine, old[m])
            b_real, b_imag = apply_band(theirs, old[m ^ bit])
            new[m] = jnp.concatenate([a_real + b_real, a_imag + b_imag], axis=0).astype(jnp.bfloat16)
        pieces = new
    order = sorted(pieces)
    n_m = len(order)
    sends = []
    codes = []
    for m in order:
        dest = side[m][2].reshape(p_dev)
        aim = side[m][3].reshape(p_dev)
        slot = dest * capacity + group_slots(dest, devices)
        pick = jnp.arange(devices * capacity, dtype=jnp.int32)[:, None] == slot[None, :]
        rows = pieces[m].reshape(2, p_dev, width).transpose(1, 0, 2).reshape(p_dev, 2 * width)
        send = jnp.dot(pick.astype(jnp.bfloat16), rows, preferred_element_type=jnp.float32)
        sends.append(send.astype(jnp.bfloat16).reshape(devices, capacity, 2 * width))
        codes.append(jnp.sum(jnp.where(pick, aim[None, :] + 1, 0), axis=1).reshape(devices, capacity))
    data = jnp.stack(sends, axis=1).reshape(devices, n_m * capacity * 2 * width)
    code = jnp.stack(codes, axis=1).reshape(devices, n_m * capacity)
    lanes = -(-2 * n_m * capacity // 128) * 128
    pad = jnp.zeros((devices, lanes - 2 * n_m * capacity), jnp.int32)
    block = jnp.concatenate([code // 32, code % 32, pad], axis=1).astype(jnp.bfloat16)
    payload = jnp.concatenate([data, block], axis=1)
    got = lax.all_to_all(payload, ("sub", "rng"), split_axis=0, concat_axis=0, tiled=True)
    size = n_m * capacity * 2 * width
    got_data = got[:, :size].reshape(n_sub, n_rng * n_m * capacity, 2 * width)
    head = got[:, size : size + n_m * capacity].astype(jnp.int32)
    low = got[:, size + n_m * capacity : size + 2 * n_m * capacity].astype(jnp.int32)
    marks = (head * 32 + low - 1).reshape(n_sub, n_rng * n_m * capacity)
    n_pieces = r_dev // width
    groups = [[] for _ in range(n_pieces)]
    for source in range(n_sub):
        index = 0
        span = n_pieces
        for section in range(section_count):
            if SPLIT[section]:
                span //= 2
                index += ((source >> section) & 1) * span
        groups[index].append(source)
    tiles = []
    for members in groups:
        block_data = jnp.concatenate([got_data[s] for s in members], axis=0)
        block_mark = jnp.concatenate([marks[s] for s in members], axis=0)
        place = (jnp.arange(p_dev, dtype=jnp.int32)[:, None] == block_mark[None, :]).astype(jnp.bfloat16)
        tile = jnp.dot(place, block_data, preferred_element_type=jnp.float32).astype(jnp.bfloat16)
        tiles.append(tile.reshape(p_dev, 2, width))
    return jnp.concatenate(tiles, axis=2).transpose(1, 0, 2)


def solution(mesh):
    in_specs = (
        P(None, "sub", "rng"),
        P(),
        P(None, "sub", None, None),
        P(None, "sub", None, None, None, None),
        P("sub", "rng", None, None),
        P("sub", "rng", None),
    )
    out_specs = P(None, "sub", "rng")
    return jax.shard_map(
        on_device, mesh=mesh, in_specs=in_specs, out_specs=out_specs, check_vma=False
    )
```

```python
import jax
import jax.numpy as jnp
from jax import lax
from jax.sharding import PartitionSpec as P

RBLK = 512


def shifted(value, axis, steps):
    count = lax.axis_size(axis)
    first, last = (max(0, -steps), min(count, count - steps))
    return lax.ppermute(value, axis, [(source, source + steps) for source in range(first, last)])


def from_partner(value, axis, apart):
    return lax.ppermute(value, axis, [(i, i ^ 1 << apart) for i in range(lax.axis_size(axis))])


def replica_matrix(chirp, block_len):
    taps_len = chirp.shape[1]
    width = block_len + taps_len
    parts = []
    for part in range(2):
        padded = jnp.concatenate([chirp[part], jnp.zeros((width + 1 - taps_len,), chirp.dtype)])
        tiled = jnp.tile(padded, block_len)[: block_len * width].reshape(block_len, width)
        parts.append(tiled.T)
    h_real, h_imag = (parts[0], parts[1])
    upper = jnp.concatenate([h_real, -h_imag], axis=1)
    lower = jnp.concatenate([h_imag, h_real], axis=1)
    return jnp.concatenate([upper, lower], axis=0)


def merge_matrix(starts, kernel):
    beams = starts.shape[0]
    taps_len = kernel.shape[-1]
    shift = jnp.arange(beams, dtype=jnp.int32)[None, :] - starts[:, None]
    g_real = jnp.zeros((beams, beams), kernel.dtype)
    g_imag = jnp.zeros((beams, beams), kernel.dtype)
    for tap in range(taps_len):
        hit = shift == tap
        g_real = jnp.where(hit, kernel[0][:, tap : tap + 1], g_real)
        g_imag = jnp.where(hit, kernel[1][:, tap : tap + 1], g_imag)
    upper = jnp.concatenate([g_real, -g_imag], axis=1)
    lower = jnp.concatenate([g_imag, g_real], axis=1)
    return jnp.concatenate([upper, lower], axis=0)


def group_slots(dest, devices):
    onehot = (dest[:, None] == jnp.arange(devices, dtype=jnp.int32)[None, :]).astype(jnp.int32)
    return jnp.sum((jnp.cumsum(onehot, axis=0) - 1) * onehot, axis=1)


def on_device(echoes, chirp, offsets, weights, owners, targets):
    p_dev = echoes.shape[1]
    r_dev = echoes.shape[2]
    n_sub = lax.axis_size("sub")
    n_rng = lax.axis_size("rng")
    devices = n_sub * n_rng
    capacity = max(2, 2 * p_dev // devices)
    tail = shifted(echoes, "rng", -1)
    extended = jnp.concatenate([echoes, tail], axis=2)
    matrix = replica_matrix(chirp, RBLK)
    stacked = jnp.concatenate([extended[0], extended[1]], axis=1)
    block_out = jnp.dot(stacked, matrix, preferred_element_type=jnp.float32).astype(jnp.bfloat16)
    pieces = block_out.reshape(p_dev, 2, RBLK)
    image = pieces.transpose(1, 0, 2).reshape(2 * p_dev, r_dev)
    section_count = offsets.shape[0]
    dest = owners.reshape(p_dev)
    aim = targets.reshape(p_dev)
    slot = dest * capacity + group_slots(dest, devices)
    pick = jnp.arange(devices * capacity, dtype=jnp.int32)[:, None] == slot[None, :]
    labels = jnp.sum(jnp.where(pick, aim[None, :] + 1, 0), axis=1) - 1
    for section in range(section_count):
        partner = from_partner(image, "sub", section)
        mine = merge_matrix(offsets[section, 0, 0], weights[section, 0, 0])
        theirs = merge_matrix(offsets[section, 0, 1], weights[section, 0, 1])
        merged = jnp.dot(mine, image, preferred_element_type=jnp.float32)
        merged = merged + jnp.dot(theirs, partner, preferred_element_type=jnp.float32)
        image = merged.astype(jnp.bfloat16)
        if section == 0:
            labels, image = lax.optimization_barrier((labels, image))
            marks = lax.all_to_all(
                labels.reshape(devices, capacity), ("sub", "rng"), split_axis=0, concat_axis=0, tiled=True
            )
    rows = image.reshape(2, p_dev, r_dev).transpose(1, 0, 2).reshape(p_dev, 2 * r_dev)
    send = jnp.dot(pick.astype(jnp.bfloat16), rows, preferred_element_type=jnp.float32).astype(
        jnp.bfloat16
    )
    got = lax.all_to_all(
        send.reshape(devices, capacity, 2 * r_dev), ("sub", "rng"), split_axis=0, concat_axis=0, tiled=True
    )
    got_flat = got.reshape(devices * capacity, 2 * r_dev)
    mark_flat = marks.reshape(devices * capacity)
    place = (jnp.arange(p_dev, dtype=jnp.int32)[:, None] == mark_flat[None, :]).astype(jnp.bfloat16)
    tile = jnp.dot(place, got_flat, preferred_element_type=jnp.float32).astype(jnp.bfloat16)
    return tile.reshape(p_dev, 2, r_dev).transpose(1, 0, 2)


def solution(mesh):
    in_specs = (
        P(None, "sub", "rng"),
        P(),
        P(None, "sub", None, None),
        P(None, "sub", None, None, None, None),
        P("sub", "rng", None, None),
        P("sub", "rng", None),
    )
    out_specs = P(None, "sub", "rng")
    return jax.shard_map(
        on_device, mesh=mesh, in_specs=in_specs, out_specs=out_specs, check_vma=False
    )
```

```python
import jax
import jax.numpy as jnp
from jax import lax
from jax.sharding import PartitionSpec as P

RBLK = 512


def shifted(value, axis, steps):
    count = lax.axis_size(axis)
    first, last = (max(0, -steps), min(count, count - steps))
    return lax.ppermute(value, axis, [(source, source + steps) for source in range(first, last)])


def from_partner(value, axis, apart):
    return lax.ppermute(value, axis, [(i, i ^ 1 << apart) for i in range(lax.axis_size(axis))])


def replica_matrix(chirp, block_len):
    taps_len = chirp.shape[1]
    width = block_len + taps_len
    parts = []
    for part in range(2):
        padded = jnp.concatenate([chirp[part], jnp.zeros((width + 1 - taps_len,), chirp.dtype)])
        tiled = jnp.tile(padded, block_len)[: block_len * width].reshape(block_len, width)
        parts.append(tiled.T)
    h_real, h_imag = (parts[0], parts[1])
    upper = jnp.concatenate([h_real, -h_imag], axis=1)
    lower = jnp.concatenate([h_imag, h_real], axis=1)
    return jnp.concatenate([upper, lower], axis=0)


def merge_matrix(starts, kernel):
    beams = starts.shape[0]
    taps_len = kernel.shape[-1]
    shift = jnp.arange(beams, dtype=jnp.int32)[None, :] - starts[:, None]
    g_real = jnp.zeros((beams, beams), kernel.dtype)
    g_imag = jnp.zeros((beams, beams), kernel.dtype)
    for tap in range(taps_len):
        hit = shift == tap
        g_real = jnp.where(hit, kernel[0][:, tap : tap + 1], g_real)
        g_imag = jnp.where(hit, kernel[1][:, tap : tap + 1], g_imag)
    upper = jnp.concatenate([g_real, -g_imag], axis=1)
    lower = jnp.concatenate([g_imag, g_real], axis=1)
    return jnp.concatenate([upper, lower], axis=0)


def group_slots(dest, devices):
    onehot = (dest[:, None] == jnp.arange(devices, dtype=jnp.int32)[None, :]).astype(jnp.int32)
    return jnp.sum((jnp.cumsum(onehot, axis=0) - 1) * onehot, axis=1)


def on_device(echoes, chirp, offsets, weights, owners, targets):
    p_dev = echoes.shape[1]
    r_dev = echoes.shape[2]
    n_sub = lax.axis_size("sub")
    n_rng = lax.axis_size("rng")
    devices = n_sub * n_rng
    capacity = max(2, 2 * p_dev // devices)
    tail = shifted(echoes, "rng", -1)
    extended = jnp.concatenate([echoes, tail], axis=2)
    matrix = replica_matrix(chirp, RBLK)
    stacked = jnp.concatenate([extended[0], extended[1]], axis=1)
    block_out = jnp.dot(stacked, matrix, preferred_element_type=jnp.float32).astype(jnp.bfloat16)
    pieces = block_out.reshape(p_dev, 2, RBLK)
    image = pieces.transpose(1, 0, 2).reshape(2 * p_dev, r_dev)
    section_count = offsets.shape[0]
    last = section_count - 1
    bit = 1 << last
    me_sub = lax.axis_index("sub")
    far = lambda value: from_partner(value, "sub", last)
    far_weights = far(weights[last, 0])
    far_ints = far(jnp.concatenate([offsets[last, 0].reshape(-1), owners.reshape(-1), targets.reshape(-1)]))
    far_offsets = far_ints[: 2 * p_dev].reshape(2, p_dev)
    far_owners = far_ints[2 * p_dev : 3 * p_dev]
    far_targets = far_ints[3 * p_dev :]
    by_group = {0: (owners.reshape(p_dev), targets.reshape(p_dev)), bit: (far_owners, far_targets)}
    picks = {}
    codes = []
    for m in (0, bit):
        dest, aim = by_group[m]
        slot = dest * capacity + group_slots(dest, devices)
        picks[m] = jnp.arange(devices * capacity, dtype=jnp.int32)[:, None] == slot[None, :]
        codes.append(jnp.sum(jnp.where(picks[m], aim[None, :] + 1, 0), axis=1).reshape(devices, capacity))
    labels = jnp.stack(codes, axis=1) - 1
    for section in range(last):
        partner = from_partner(image, "sub", section)
        mine = merge_matrix(offsets[section, 0, 0], weights[section, 0, 0])
        theirs = merge_matrix(offsets[section, 0, 1], weights[section, 0, 1])
        merged = jnp.dot(mine, image, preferred_element_type=jnp.float32)
        merged = merged + jnp.dot(theirs, partner, preferred_element_type=jnp.float32)
        image = merged.astype(jnp.bfloat16)
        if section == 0:
            labels, image = lax.optimization_barrier((labels, image))
            marks = lax.all_to_all(labels, ("sub", "rng"), split_axis=0, concat_axis=0, tiled=True)
    half = r_dev // 2
    keep_bit = (me_sub >> last) & 1
    kept = lax.dynamic_slice_in_dim(image, keep_bit * half, half, axis=1)
    sent = lax.dynamic_slice_in_dim(image, (1 - keep_bit) * half, half, axis=1)
    old = {0: kept, bit: far(sent)}
    bands = {
        0: (offsets[last, 0], weights[last, 0]),
        bit: (far_offsets, far_weights),
    }
    sends = []
    for m in (0, bit):
        starts, kernel = bands[m]
        mine = merge_matrix(starts[0], kernel[0])
        theirs = merge_matrix(starts[1], kernel[1])
        merged = jnp.dot(mine, old[m], preferred_element_type=jnp.float32)
        merged = merged + jnp.dot(theirs, old[m ^ bit], preferred_element_type=jnp.float32)
        piece = merged.astype(jnp.bfloat16)
        rows = piece.reshape(2, p_dev, half).transpose(1, 0, 2).reshape(p_dev, 2 * half)
        send = jnp.dot(picks[m].astype(jnp.bfloat16), rows, preferred_element_type=jnp.float32)
        sends.append(send.astype(jnp.bfloat16).reshape(devices, capacity, 2 * half))
    payload = jnp.concatenate(sends, axis=1)
    got = lax.all_to_all(payload, ("sub", "rng"), split_axis=0, concat_axis=0, tiled=True)
    span = devices // 2
    tiles = []
    for h in range(2):
        sources = [s for s in range(n_sub) if (s >> last) & 1 == h]
        block_data = jnp.concatenate(
            [got[s * n_rng : (s + 1) * n_rng] for s in sources], axis=0
        ).reshape(span * 2 * capacity, 2 * half)
        block_mark = jnp.concatenate(
            [marks[s * n_rng : (s + 1) * n_rng] for s in sources], axis=0
        ).reshape(span * 2 * capacity)
        place = (jnp.arange(p_dev, dtype=jnp.int32)[:, None] == block_mark[None, :]).astype(jnp.bfloat16)
        tile = jnp.dot(place, block_data, preferred_element_type=jnp.float32).astype(jnp.bfloat16)
        tiles.append(tile.reshape(p_dev, 2, half))
    return jnp.concatenate(tiles, axis=2).transpose(1, 0, 2)


def solution(mesh):
    in_specs = (
        P(None, "sub", "rng"),
        P(),
        P(None, "sub", None, None),
        P(None, "sub", None, None, None, None),
        P("sub", "rng", None, None),
        P("sub", "rng", None),
    )
    out_specs = P(None, "sub", "rng")
    return jax.shard_map(
        on_device, mesh=mesh, in_specs=in_specs, out_specs=out_specs, check_vma=False
    )
```

```python
import jax
import jax.numpy as jnp
from jax import lax
from jax.sharding import PartitionSpec as P

RBLK = 512


def shifted(value, axis, steps):
    count = lax.axis_size(axis)
    first, last = (max(0, -steps), min(count, count - steps))
    return lax.ppermute(value, axis, [(source, source + steps) for source in range(first, last)])


def from_partner(value, axis, apart):
    return lax.ppermute(value, axis, [(i, i ^ 1 << apart) for i in range(lax.axis_size(axis))])


def replica_matrix(chirp, block_len):
    taps_len = chirp.shape[1]
    width = block_len + taps_len
    parts = []
    for part in range(2):
        padded = jnp.concatenate([chirp[part], jnp.zeros((width + 1 - taps_len,), chirp.dtype)])
        tiled = jnp.tile(padded, block_len)[: block_len * width].reshape(block_len, width)
        parts.append(tiled.T)
    h_real, h_imag = (parts[0], parts[1])
    upper = jnp.concatenate([h_real, -h_imag], axis=1)
    lower = jnp.concatenate([h_imag, h_real], axis=1)
    return jnp.concatenate([upper, lower], axis=0)


def merge_matrix(starts, kernel):
    beams = starts.shape[0]
    taps_len = kernel.shape[-1]
    shift = jnp.arange(beams, dtype=jnp.int32)[None, :] - starts[:, None]
    g_real = jnp.zeros((beams, beams), kernel.dtype)
    g_imag = jnp.zeros((beams, beams), kernel.dtype)
    for tap in range(taps_len):
        hit = shift == tap
        g_real = jnp.where(hit, kernel[0][:, tap : tap + 1], g_real)
        g_imag = jnp.where(hit, kernel[1][:, tap : tap + 1], g_imag)
    upper = jnp.concatenate([g_real, -g_imag], axis=1)
    lower = jnp.concatenate([g_imag, g_real], axis=1)
    return jnp.concatenate([upper, lower], axis=0)


def group_slots(dest, devices):
    onehot = (dest[:, None] == jnp.arange(devices, dtype=jnp.int32)[None, :]).astype(jnp.int32)
    return jnp.sum((jnp.cumsum(onehot, axis=0) - 1) * onehot, axis=1)


def on_device(echoes, chirp, offsets, weights, owners, targets):
    p_dev = echoes.shape[1]
    r_dev = echoes.shape[2]
    n_sub = lax.axis_size("sub")
    n_rng = lax.axis_size("rng")
    devices = n_sub * n_rng
    capacity = max(2, 2 * p_dev // devices)
    tail = shifted(echoes, "rng", -1)
    extended = jnp.concatenate([echoes, tail], axis=2)
    matrix = replica_matrix(chirp, RBLK)
    stacked = jnp.concatenate([extended[0], extended[1]], axis=1)
    block_out = jnp.dot(stacked, matrix, preferred_element_type=jnp.float32).astype(jnp.bfloat16)
    pieces = block_out.reshape(p_dev, 2, RBLK)
    image = pieces.transpose(1, 0, 2).reshape(2 * p_dev, r_dev)
    section_count = offsets.shape[0]
    last = section_count - 1
    bit = 1 << last
    me_sub = lax.axis_index("sub")
    far = lambda value: from_partner(value, "sub", last)
    far_weights = far(weights[last, 0])
    far_ints = far(jnp.concatenate([offsets[last, 0].reshape(-1), owners.reshape(-1), targets.reshape(-1)]))
    far_offsets = far_ints[: 2 * p_dev].reshape(2, p_dev)
    far_owners = far_ints[2 * p_dev : 3 * p_dev]
    far_targets = far_ints[3 * p_dev :]
    by_group = {0: (owners.reshape(p_dev), targets.reshape(p_dev)), bit: (far_owners, far_targets)}
    picks = {}
    codes = []
    for m in (0, bit):
        dest, aim = by_group[m]
        slot = dest * capacity + group_slots(dest, devices)
        picks[m] = jnp.arange(devices * capacity, dtype=jnp.int32)[:, None] == slot[None, :]
        codes.append(jnp.sum(jnp.where(picks[m], aim[None, :] + 1, 0), axis=1).reshape(devices, capacity))
    labels = jnp.stack(codes, axis=1) - 1
    late = (offsets[1:], weights[1:], far_offsets, far_weights)
    late, image = lax.optimization_barrier((late, image))
    late_offsets, late_weights, far_offsets, far_weights = late
    offsets = jnp.concatenate([offsets[:1], late_offsets], axis=0)
    weights = jnp.concatenate([weights[:1], late_weights], axis=0)
    for section in range(last):
        partner = from_partner(image, "sub", section)
        mine = merge_matrix(offsets[section, 0, 0], weights[section, 0, 0])
        theirs = merge_matrix(offsets[section, 0, 1], weights[section, 0, 1])
        merged = jnp.dot(mine, image, preferred_element_type=jnp.float32)
        merged = merged + jnp.dot(theirs, partner, preferred_element_type=jnp.float32)
        image = merged.astype(jnp.bfloat16)
        if section == 0:
            labels, image = lax.optimization_barrier((labels, image))
            marks = lax.all_to_all(labels, ("sub", "rng"), split_axis=0, concat_axis=0, tiled=True)
        if section == 1:
            marks, image = lax.optimization_barrier((marks, image))
    half = r_dev // 2
    keep_bit = (me_sub >> last) & 1
    kept = lax.dynamic_slice_in_dim(image, keep_bit * half, half, axis=1)
    sent = lax.dynamic_slice_in_dim(image, (1 - keep_bit) * half, half, axis=1)
    old = {0: kept, bit: far(sent)}
    bands = {
        0: (offsets[last, 0], weights[last, 0]),
        bit: (far_offsets, far_weights),
    }
    sends = []
    for m in (0, bit):
        starts, kernel = bands[m]
        mine = merge_matrix(starts[0], kernel[0])
        theirs = merge_matrix(starts[1], kernel[1])
        merged = jnp.dot(mine, old[m], preferred_element_type=jnp.float32)
        merged = merged + jnp.dot(theirs, old[m ^ bit], preferred_element_type=jnp.float32)
        piece = merged.astype(jnp.bfloat16)
        rows = piece.reshape(2, p_dev, half).transpose(1, 0, 2).reshape(p_dev, 2 * half)
        send = jnp.dot(picks[m].astype(jnp.bfloat16), rows, preferred_element_type=jnp.float32)
        sends.append(send.astype(jnp.bfloat16).reshape(devices, capacity, 2 * half))
    payload = jnp.concatenate(sends, axis=1)
    got = lax.all_to_all(payload, ("sub", "rng"), split_axis=0, concat_axis=0, tiled=True)
    span = devices // 2
    tiles = []
    for h in range(2):
        sources = [s for s in range(n_sub) if (s >> last) & 1 == h]
        block_data = jnp.concatenate(
            [got[s * n_rng : (s + 1) * n_rng] for s in sources], axis=0
        ).reshape(span * 2 * capacity, 2 * half)
        block_mark = jnp.concatenate(
            [marks[s * n_rng : (s + 1) * n_rng] for s in sources], axis=0
        ).reshape(span * 2 * capacity)
        place = (jnp.arange(p_dev, dtype=jnp.int32)[:, None] == block_mark[None, :]).astype(jnp.bfloat16)
        tile = jnp.dot(place, block_data, preferred_element_type=jnp.float32).astype(jnp.bfloat16)
        tiles.append(tile.reshape(p_dev, 2, half))
    return jnp.concatenate(tiles, axis=2).transpose(1, 0, 2)


def solution(mesh):
    in_specs = (
        P(None, "sub", "rng"),
        P(),
        P(None, "sub", None, None),
        P(None, "sub", None, None, None, None),
        P("sub", "rng", None, None),
        P("sub", "rng", None),
    )
    out_specs = P(None, "sub", "rng")
    return jax.shard_map(
        on_device, mesh=mesh, in_specs=in_specs, out_specs=out_specs, check_vma=False
    )
```

```python
import jax
import jax.numpy as jnp
from jax import lax
from jax.sharding import PartitionSpec as P

RBLK = 512


def shifted(value, axis, steps):
    count = lax.axis_size(axis)
    first, last = (max(0, -steps), min(count, count - steps))
    return lax.ppermute(value, axis, [(source, source + steps) for source in range(first, last)])


def from_partner(value, axis, apart):
    return lax.ppermute(value, axis, [(i, i ^ 1 << apart) for i in range(lax.axis_size(axis))])


def replica_matrix(chirp, block_len):
    taps_len = chirp.shape[1]
    width = block_len + taps_len
    parts = []
    for part in range(2):
        padded = jnp.concatenate([chirp[part], jnp.zeros((width + 1 - taps_len,), chirp.dtype)])
        tiled = jnp.tile(padded, block_len)[: block_len * width].reshape(block_len, width)
        parts.append(tiled.T)
    h_real, h_imag = (parts[0], parts[1])
    upper = jnp.concatenate([h_real, -h_imag], axis=1)
    lower = jnp.concatenate([h_imag, h_real], axis=1)
    return jnp.concatenate([upper, lower], axis=0)


def merge_matrix(starts, kernel):
    beams = starts.shape[0]
    taps_len = kernel.shape[-1]
    shift = jnp.arange(beams, dtype=jnp.int32)[None, :] - starts[:, None]
    g_real = jnp.zeros((beams, beams), kernel.dtype)
    g_imag = jnp.zeros((beams, beams), kernel.dtype)
    for tap in range(taps_len):
        hit = shift == tap
        g_real = jnp.where(hit, kernel[0][:, tap : tap + 1], g_real)
        g_imag = jnp.where(hit, kernel[1][:, tap : tap + 1], g_imag)
    upper = jnp.concatenate([g_real, -g_imag], axis=1)
    lower = jnp.concatenate([g_imag, g_real], axis=1)
    return jnp.concatenate([upper, lower], axis=0)


def group_slots(dest, devices):
    onehot = (dest[:, None] == jnp.arange(devices, dtype=jnp.int32)[None, :]).astype(jnp.int32)
    return jnp.sum((jnp.cumsum(onehot, axis=0) - 1) * onehot, axis=1)


def on_device(echoes, chirp, offsets, weights, owners, targets):
    p_dev = echoes.shape[1]
    r_dev = echoes.shape[2]
    n_sub = lax.axis_size("sub")
    n_rng = lax.axis_size("rng")
    devices = n_sub * n_rng
    capacity = max(2, 2 * p_dev // devices)
    tail = shifted(echoes, "rng", -1)
    extended = jnp.concatenate([echoes, tail], axis=2)
    matrix = replica_matrix(chirp, RBLK)
    stacked = jnp.concatenate([extended[0], extended[1]], axis=1)
    block_out = jnp.dot(stacked, matrix, preferred_element_type=jnp.float32).astype(jnp.bfloat16)
    pieces = block_out.reshape(p_dev, 2, RBLK)
    image = pieces.transpose(1, 0, 2).reshape(2 * p_dev, r_dev)
    section_count = offsets.shape[0]
    last = section_count - 1
    bit = 1 << last
    me_sub = lax.axis_index("sub")
    far = lambda value: from_partner(value, "sub", last)
    dest = owners.reshape(p_dev)
    aim = targets.reshape(p_dev)
    slot = dest * capacity + group_slots(dest, devices)
    pick = jnp.arange(devices * capacity, dtype=jnp.int32)[:, None] == slot[None, :]
    labels = jnp.sum(jnp.where(pick, aim[None, :] + 1, 0), axis=1).reshape(devices, capacity) - 1
    late = (offsets[last, 0], weights[last, 0], slot)
    for section in range(last):
        partner = from_partner(image, "sub", section)
        mine = merge_matrix(offsets[section, 0, 0], weights[section, 0, 0])
        theirs = merge_matrix(offsets[section, 0, 1], weights[section, 0, 1])
        merged = jnp.dot(mine, image, preferred_element_type=jnp.float32)
        merged = merged + jnp.dot(theirs, partner, preferred_element_type=jnp.float32)
        image = merged.astype(jnp.bfloat16)
        if section == 0:
            (labels, late), image = lax.optimization_barrier(((labels, late), image))
            marks = lax.all_to_all(labels, ("sub", "rng"), split_axis=0, concat_axis=0, tiled=True)
            own_offsets, own_weights, slot = late
            far_weights = far(own_weights)
            far_ints = far(jnp.concatenate([own_offsets.reshape(-1), slot]))
            far_offsets = far_ints[: 2 * p_dev].reshape(2, p_dev)
            far_slot = far_ints[2 * p_dev :]
        if section == 1:
            marks, image = lax.optimization_barrier((marks, image))
    slots = jnp.arange(devices * capacity, dtype=jnp.int32)[:, None]
    picks = {0: slots == slot[None, :], bit: slots == far_slot[None, :]}
    grid = marks.reshape(n_sub, n_rng * capacity)
    swapped = jnp.stack([grid[s ^ bit] for s in range(n_sub)], axis=0)
    marks = jnp.stack(
        [grid.reshape(devices, capacity), swapped.reshape(devices, capacity)], axis=1
    ).reshape(devices, 2 * capacity)
    half = r_dev // 2
    keep_bit = (me_sub >> last) & 1
    kept = lax.dynamic_slice_in_dim(image, keep_bit * half, half, axis=1)
    sent = lax.dynamic_slice_in_dim(image, (1 - keep_bit) * half, half, axis=1)
    old = {0: kept, bit: far(sent)}
    bands = {
        0: (own_offsets, own_weights),
        bit: (far_offsets, far_weights),
    }
    sends = []
    for m in (0, bit):
        starts, kernel = bands[m]
        mine = merge_matrix(starts[0], kernel[0])
        theirs = merge_matrix(starts[1], kernel[1])
        merged = jnp.dot(mine, old[m], preferred_element_type=jnp.float32)
        merged = merged + jnp.dot(theirs, old[m ^ bit], preferred_element_type=jnp.float32)
        piece = merged.astype(jnp.bfloat16)
        rows = piece.reshape(2, p_dev, half).transpose(1, 0, 2).reshape(p_dev, 2 * half)
        send = jnp.dot(picks[m].astype(jnp.bfloat16), rows, preferred_element_type=jnp.float32)
        sends.append(send.astype(jnp.bfloat16).reshape(devices, capacity, 2 * half))
    payload = jnp.concatenate(sends, axis=1)
    got = lax.all_to_all(payload, ("sub", "rng"), split_axis=0, concat_axis=0, tiled=True)
    span = devices // 2
    tiles = []
    for h in range(2):
        sources = [s for s in range(n_sub) if (s >> last) & 1 == h]
        block_data = jnp.concatenate(
            [got[s * n_rng : (s + 1) * n_rng] for s in sources], axis=0
        ).reshape(span * 2 * capacity, 2 * half)
        block_mark = jnp.concatenate(
            [marks[s * n_rng : (s + 1) * n_rng] for s in sources], axis=0
        ).reshape(span * 2 * capacity)
        place = (jnp.arange(p_dev, dtype=jnp.int32)[:, None] == block_mark[None, :]).astype(jnp.bfloat16)
        tile = jnp.dot(place, block_data, preferred_element_type=jnp.float32).astype(jnp.bfloat16)
        tiles.append(tile.reshape(p_dev, 2, half))
    return jnp.concatenate(tiles, axis=2).transpose(1, 0, 2)


def solution(mesh):
    in_specs = (
        P(None, "sub", "rng"),
        P(),
        P(None, "sub", None, None),
        P(None, "sub", None, None, None, None),
        P("sub", "rng", None, None),
        P("sub", "rng", None),
    )
    out_specs = P(None, "sub", "rng")
    return jax.shard_map(
        on_device, mesh=mesh, in_specs=in_specs, out_specs=out_specs, check_vma=False
    )
```

```python
import jax
import jax.numpy as jnp
from jax import lax
from jax.sharding import PartitionSpec as P

RBLK = 512


def shifted(value, axis, steps):
    count = lax.axis_size(axis)
    first, last = (max(0, -steps), min(count, count - steps))
    return lax.ppermute(value, axis, [(source, source + steps) for source in range(first, last)])


def from_partner(value, axis, apart):
    return lax.ppermute(value, axis, [(i, i ^ 1 << apart) for i in range(lax.axis_size(axis))])


def replica_matrix(chirp, block_len):
    taps_len = chirp.shape[1]
    width = block_len + taps_len
    parts = []
    for part in range(2):
        padded = jnp.concatenate([chirp[part], jnp.zeros((width + 1 - taps_len,), chirp.dtype)])
        tiled = jnp.tile(padded, block_len)[: block_len * width].reshape(block_len, width)
        parts.append(tiled.T)
    h_real, h_imag = (parts[0], parts[1])
    upper = jnp.concatenate([h_real, -h_imag], axis=1)
    lower = jnp.concatenate([h_imag, h_real], axis=1)
    return jnp.concatenate([upper, lower], axis=0)


def merge_matrix(starts, kernel):
    beams = starts.shape[0]
    taps_len = kernel.shape[-1]
    shift = jnp.arange(beams, dtype=jnp.int32)[None, :] - starts[:, None]
    g_real = jnp.zeros((beams, beams), kernel.dtype)
    g_imag = jnp.zeros((beams, beams), kernel.dtype)
    for tap in range(taps_len):
        hit = shift == tap
        g_real = jnp.where(hit, kernel[0][:, tap : tap + 1], g_real)
        g_imag = jnp.where(hit, kernel[1][:, tap : tap + 1], g_imag)
    upper = jnp.concatenate([g_real, -g_imag], axis=1)
    lower = jnp.concatenate([g_imag, g_real], axis=1)
    return jnp.concatenate([upper, lower], axis=0)


def group_slots(dest, devices):
    onehot = (dest[:, None] == jnp.arange(devices, dtype=jnp.int32)[None, :]).astype(jnp.int32)
    return jnp.sum((jnp.cumsum(onehot, axis=0) - 1) * onehot, axis=1)


def on_device(echoes, chirp, offsets, weights, owners, targets):
    p_dev = echoes.shape[1]
    r_dev = echoes.shape[2]
    n_sub = lax.axis_size("sub")
    n_rng = lax.axis_size("rng")
    devices = n_sub * n_rng
    capacity = max(2, 2 * p_dev // devices)
    tail = shifted(echoes, "rng", -1)
    extended = jnp.concatenate([echoes, tail], axis=2)
    matrix = replica_matrix(chirp, RBLK)
    stacked = jnp.concatenate([extended[0], extended[1]], axis=1)
    block_out = jnp.dot(stacked, matrix, preferred_element_type=jnp.float32).astype(jnp.bfloat16)
    pieces = block_out.reshape(p_dev, 2, RBLK)
    image = pieces.transpose(1, 0, 2).reshape(2 * p_dev, r_dev)
    section_count = offsets.shape[0]
    last = section_count - 1
    bit = 1 << last
    me_sub = lax.axis_index("sub")
    far = lambda value: from_partner(value, "sub", last)
    dest = owners.reshape(p_dev)
    aim = targets.reshape(p_dev)
    slot = dest * capacity + group_slots(dest, devices)
    pick = jnp.arange(devices * capacity, dtype=jnp.int32)[:, None] == slot[None, :]
    labels = jnp.sum(jnp.where(pick, aim[None, :] + 1, 0), axis=1).reshape(devices, capacity) - 1
    late = (offsets[last, 0], weights[last, 0], slot)
    for section in range(last):
        partner = from_partner(image, "sub", section)
        mine = merge_matrix(offsets[section, 0, 0], weights[section, 0, 0])
        theirs = merge_matrix(offsets[section, 0, 1], weights[section, 0, 1])
        merged = jnp.dot(mine, image, preferred_element_type=jnp.float32)
        if section == 1:
            (labels, late), merged = lax.optimization_barrier(((labels, late), merged))
            marks = lax.all_to_all(labels, ("sub", "rng"), split_axis=0, concat_axis=0, tiled=True)
            own_offsets, own_weights, slot = late
            far_weights = far(own_weights)
            far_ints = far(jnp.concatenate([own_offsets.reshape(-1), slot]))
            far_offsets = far_ints[: 2 * p_dev].reshape(2, p_dev)
            far_slot = far_ints[2 * p_dev :]
        merged = merged + jnp.dot(theirs, partner, preferred_element_type=jnp.float32)
        image = merged.astype(jnp.bfloat16)
        if section == 1:
            marks, image = lax.optimization_barrier((marks, image))
    slots = jnp.arange(devices * capacity, dtype=jnp.int32)[:, None]
    picks = {0: slots == slot[None, :], bit: slots == far_slot[None, :]}
    grid = marks.reshape(n_sub, n_rng * capacity)
    swapped = jnp.stack([grid[s ^ bit] for s in range(n_sub)], axis=0)
    marks = jnp.stack(
        [grid.reshape(devices, capacity), swapped.reshape(devices, capacity)], axis=1
    ).reshape(devices, 2 * capacity)
    half = r_dev // 2
    keep_bit = (me_sub >> last) & 1
    kept = lax.dynamic_slice_in_dim(image, keep_bit * half, half, axis=1)
    sent = lax.dynamic_slice_in_dim(image, (1 - keep_bit) * half, half, axis=1)
    old = {0: kept, bit: far(sent)}
    bands = {
        0: (own_offsets, own_weights),
        bit: (far_offsets, far_weights),
    }
    sends = []
    for m in (0, bit):
        starts, kernel = bands[m]
        mine = merge_matrix(starts[0], kernel[0])
        theirs = merge_matrix(starts[1], kernel[1])
        merged = jnp.dot(mine, old[m], preferred_element_type=jnp.float32)
        merged = merged + jnp.dot(theirs, old[m ^ bit], preferred_element_type=jnp.float32)
        piece = merged.astype(jnp.bfloat16)
        rows = piece.reshape(2, p_dev, half).transpose(1, 0, 2).reshape(p_dev, 2 * half)
        send = jnp.dot(picks[m].astype(jnp.bfloat16), rows, preferred_element_type=jnp.float32)
        sends.append(send.astype(jnp.bfloat16).reshape(devices, capacity, 2 * half))
    payload = jnp.concatenate(sends, axis=1)
    got = lax.all_to_all(payload, ("sub", "rng"), split_axis=0, concat_axis=0, tiled=True)
    span = devices // 2
    tiles = []
    for h in range(2):
        sources = [s for s in range(n_sub) if (s >> last) & 1 == h]
        block_data = jnp.concatenate(
            [got[s * n_rng : (s + 1) * n_rng] for s in sources], axis=0
        ).reshape(span * 2 * capacity, 2 * half)
        block_mark = jnp.concatenate(
            [marks[s * n_rng : (s + 1) * n_rng] for s in sources], axis=0
        ).reshape(span * 2 * capacity)
        place = (jnp.arange(p_dev, dtype=jnp.int32)[:, None] == block_mark[None, :]).astype(jnp.bfloat16)
        tile = jnp.dot(place, block_data, preferred_element_type=jnp.float32).astype(jnp.bfloat16)
        tiles.append(tile.reshape(p_dev, 2, half))
    return jnp.concatenate(tiles, axis=2).transpose(1, 0, 2)


def solution(mesh):
    in_specs = (
        P(None, "sub", "rng"),
        P(),
        P(None, "sub", None, None),
        P(None, "sub", None, None, None, None),
        P("sub", "rng", None, None),
        P("sub", "rng", None),
    )
    out_specs = P(None, "sub", "rng")
    return jax.shard_map(
        on_device, mesh=mesh, in_specs=in_specs, out_specs=out_specs, check_vma=False
    )
```

```python
import jax
import jax.numpy as jnp
from jax import lax
from jax.sharding import PartitionSpec as P

RBLK = 512


def shifted(value, axis, steps):
    count = lax.axis_size(axis)
    first, last = (max(0, -steps), min(count, count - steps))
    return lax.ppermute(value, axis, [(source, source + steps) for source in range(first, last)])


def from_partner(value, axis, apart):
    return lax.ppermute(value, axis, [(i, i ^ 1 << apart) for i in range(lax.axis_size(axis))])


def replica_matrix(chirp, block_len):
    taps_len = chirp.shape[1]
    width = block_len + taps_len
    parts = []
    for part in range(2):
        padded = jnp.concatenate([chirp[part], jnp.zeros((width + 1 - taps_len,), chirp.dtype)])
        tiled = jnp.tile(padded, block_len)[: block_len * width].reshape(block_len, width)
        parts.append(tiled.T)
    h_real, h_imag = (parts[0], parts[1])
    upper = jnp.concatenate([h_real, -h_imag], axis=1)
    lower = jnp.concatenate([h_imag, h_real], axis=1)
    return jnp.concatenate([upper, lower], axis=0)


def merge_matrix(starts, kernel):
    beams = starts.shape[0]
    taps_len = kernel.shape[-1]
    shift = jnp.arange(beams, dtype=jnp.int32)[None, :] - starts[:, None]
    g_real = jnp.zeros((beams, beams), kernel.dtype)
    g_imag = jnp.zeros((beams, beams), kernel.dtype)
    for tap in range(taps_len):
        hit = shift == tap
        g_real = jnp.where(hit, kernel[0][:, tap : tap + 1], g_real)
        g_imag = jnp.where(hit, kernel[1][:, tap : tap + 1], g_imag)
    upper = jnp.concatenate([g_real, -g_imag], axis=1)
    lower = jnp.concatenate([g_imag, g_real], axis=1)
    return jnp.concatenate([upper, lower], axis=0)


def group_slots(dest, devices):
    onehot = (dest[:, None] == jnp.arange(devices, dtype=jnp.int32)[None, :]).astype(jnp.int32)
    return jnp.sum((jnp.cumsum(onehot, axis=0) - 1) * onehot, axis=1)


def on_device(echoes, chirp, offsets, weights, owners, targets):
    p_dev = echoes.shape[1]
    r_dev = echoes.shape[2]
    n_sub = lax.axis_size("sub")
    n_rng = lax.axis_size("rng")
    devices = n_sub * n_rng
    capacity = max(2, 2 * p_dev // devices)
    tail = shifted(echoes, "rng", -1)
    extended = jnp.concatenate([echoes, tail], axis=2)
    matrix = replica_matrix(chirp, RBLK)
    stacked = jnp.concatenate([extended[0], extended[1]], axis=1)
    block_out = jnp.dot(stacked, matrix, preferred_element_type=jnp.float32).astype(jnp.bfloat16)
    pieces = block_out.reshape(p_dev, 2, RBLK)
    image = pieces.transpose(1, 0, 2).reshape(2 * p_dev, r_dev)
    section_count = offsets.shape[0]
    last = section_count - 1
    bit = 1 << last
    me_sub = lax.axis_index("sub")
    far = lambda value: from_partner(value, "sub", last)
    dest = owners.reshape(p_dev)
    aim = targets.reshape(p_dev)
    slot = dest * capacity + group_slots(dest, devices)
    pick = jnp.arange(devices * capacity, dtype=jnp.int32)[:, None] == slot[None, :]
    labels = jnp.sum(jnp.where(pick, aim[None, :] + 1, 0), axis=1).reshape(devices, capacity) - 1
    late = (offsets[last, 0], weights[last, 0], slot)
    for section in range(last):
        partner = from_partner(image, "sub", section)
        mine = merge_matrix(offsets[section, 0, 0], weights[section, 0, 0])
        theirs = merge_matrix(offsets[section, 0, 1], weights[section, 0, 1])
        merged = jnp.dot(mine, image, preferred_element_type=jnp.float32)
        if section == 1:
            late, merged = lax.optimization_barrier((late, merged))
            own_offsets, own_weights, slot = late
            far_weights = far(own_weights)
            far_ints = far(jnp.concatenate([own_offsets.reshape(-1), slot]))
            far_offsets = far_ints[: 2 * p_dev].reshape(2, p_dev)
            far_slot = far_ints[2 * p_dev :]
        merged = merged + jnp.dot(theirs, partner, preferred_element_type=jnp.float32)
        image = merged.astype(jnp.bfloat16)
    slots = jnp.arange(devices * capacity, dtype=jnp.int32)[:, None]
    picks = {0: slots == slot[None, :], bit: slots == far_slot[None, :]}
    half = r_dev // 2
    keep_bit = (me_sub >> last) & 1
    kept = lax.dynamic_slice_in_dim(image, keep_bit * half, half, axis=1)
    sent = lax.dynamic_slice_in_dim(image, (1 - keep_bit) * half, half, axis=1)
    old = {0: kept, bit: far(sent)}
    bands = {
        0: (own_offsets, own_weights),
        bit: (far_offsets, far_weights),
    }
    sends = []
    for m in (0, bit):
        starts, kernel = bands[m]
        mine = merge_matrix(starts[0], kernel[0])
        theirs = merge_matrix(starts[1], kernel[1])
        merged = jnp.dot(mine, old[m], preferred_element_type=jnp.float32)
        if m == 0:
            labels, merged = lax.optimization_barrier((labels, merged))
            marks = lax.all_to_all(labels, ("sub", "rng"), split_axis=0, concat_axis=0, tiled=True)
        merged = merged + jnp.dot(theirs, old[m ^ bit], preferred_element_type=jnp.float32)
        piece = merged.astype(jnp.bfloat16)
        rows = piece.reshape(2, p_dev, half).transpose(1, 0, 2).reshape(p_dev, 2 * half)
        send = jnp.dot(picks[m].astype(jnp.bfloat16), rows, preferred_element_type=jnp.float32)
        sends.append(send.astype(jnp.bfloat16).reshape(devices, capacity, 2 * half))
    grid = marks.reshape(n_sub, n_rng * capacity)
    swapped = jnp.stack([grid[s ^ bit] for s in range(n_sub)], axis=0)
    marks = jnp.stack(
        [grid.reshape(devices, capacity), swapped.reshape(devices, capacity)], axis=1
    ).reshape(devices, 2 * capacity)
    payload = jnp.concatenate(sends, axis=1)
    got = lax.all_to_all(payload, ("sub", "rng"), split_axis=0, concat_axis=0, tiled=True)
    span = devices // 2
    tiles = []
    for h in range(2):
        sources = [s for s in range(n_sub) if (s >> last) & 1 == h]
        block_data = jnp.concatenate(
            [got[s * n_rng : (s + 1) * n_rng] for s in sources], axis=0
        ).reshape(span * 2 * capacity, 2 * half)
        block_mark = jnp.concatenate(
            [marks[s * n_rng : (s + 1) * n_rng] for s in sources], axis=0
        ).reshape(span * 2 * capacity)
        place = (jnp.arange(p_dev, dtype=jnp.int32)[:, None] == block_mark[None, :]).astype(jnp.bfloat16)
        tile = jnp.dot(place, block_data, preferred_element_type=jnp.float32).astype(jnp.bfloat16)
        tiles.append(tile.reshape(p_dev, 2, half))
    return jnp.concatenate(tiles, axis=2).transpose(1, 0, 2)


def solution(mesh):
    in_specs = (
        P(None, "sub", "rng"),
        P(),
        P(None, "sub", None, None),
        P(None, "sub", None, None, None, None),
        P("sub", "rng", None, None),
        P("sub", "rng", None),
    )
    out_specs = P(None, "sub", "rng")
    return jax.shard_map(
        on_device, mesh=mesh, in_specs=in_specs, out_specs=out_specs, check_vma=False
    )
```

```python
import jax
import jax.numpy as jnp
from jax import lax
from jax.sharding import PartitionSpec as P

RBLK = 512


def shifted(value, axis, steps):
    count = lax.axis_size(axis)
    first, last = (max(0, -steps), min(count, count - steps))
    return lax.ppermute(value, axis, [(source, source + steps) for source in range(first, last)])


def from_partner(value, axis, apart):
    return lax.ppermute(value, axis, [(i, i ^ 1 << apart) for i in range(lax.axis_size(axis))])


def replica_matrix(chirp, block_len):
    taps_len = chirp.shape[1]
    width = block_len + taps_len
    parts = []
    for part in range(2):
        padded = jnp.concatenate([chirp[part], jnp.zeros((width + 1 - taps_len,), chirp.dtype)])
        tiled = jnp.tile(padded, block_len)[: block_len * width].reshape(block_len, width)
        parts.append(tiled.T)
    h_real, h_imag = (parts[0], parts[1])
    upper = jnp.concatenate([h_real, -h_imag], axis=1)
    lower = jnp.concatenate([h_imag, h_real], axis=1)
    return jnp.concatenate([upper, lower], axis=0)


def merge_matrix(starts, kernel):
    beams = starts.shape[0]
    taps_len = kernel.shape[-1]
    shift = jnp.arange(beams, dtype=jnp.int32)[None, :] - starts[:, None]
    g_real = jnp.zeros((beams, beams), kernel.dtype)
    g_imag = jnp.zeros((beams, beams), kernel.dtype)
    for tap in range(taps_len):
        hit = shift == tap
        g_real = jnp.where(hit, kernel[0][:, tap : tap + 1], g_real)
        g_imag = jnp.where(hit, kernel[1][:, tap : tap + 1], g_imag)
    upper = jnp.concatenate([g_real, -g_imag], axis=1)
    lower = jnp.concatenate([g_imag, g_real], axis=1)
    return jnp.concatenate([upper, lower], axis=0)


def group_slots(dest, devices):
    onehot = (dest[:, None] == jnp.arange(devices, dtype=jnp.int32)[None, :]).astype(jnp.int32)
    return jnp.sum((jnp.cumsum(onehot, axis=0) - 1) * onehot, axis=1)


def on_device(echoes, chirp, offsets, weights, owners, targets):
    p_dev = echoes.shape[1]
    r_dev = echoes.shape[2]
    n_sub = lax.axis_size("sub")
    n_rng = lax.axis_size("rng")
    devices = n_sub * n_rng
    capacity = max(2, 2 * p_dev // devices)
    tail = shifted(echoes, "rng", -1)
    extended = jnp.concatenate([echoes, tail], axis=2)
    matrix = replica_matrix(chirp, RBLK)
    late = (offsets[-1, 0], weights[-1, 0], owners, targets)
    late, matrix = lax.optimization_barrier((late, matrix))
    stacked = jnp.concatenate([extended[0], extended[1]], axis=1)
    block_out = jnp.dot(stacked, matrix, preferred_element_type=jnp.float32).astype(jnp.bfloat16)
    pieces = block_out.reshape(p_dev, 2, RBLK)
    image = pieces.transpose(1, 0, 2).reshape(2 * p_dev, r_dev)
    section_count = offsets.shape[0]
    last = section_count - 1
    bit = 1 << last
    me_sub = lax.axis_index("sub")
    far = lambda value: from_partner(value, "sub", last)
    own_offsets, own_weights, owners, targets = late
    dest = owners.reshape(p_dev)
    aim = targets.reshape(p_dev)
    slot = dest * capacity + group_slots(dest, devices)
    pick = jnp.arange(devices * capacity, dtype=jnp.int32)[:, None] == slot[None, :]
    labels = jnp.sum(jnp.where(pick, aim[None, :] + 1, 0), axis=1).reshape(devices, capacity) - 1
    far_weights = far(own_weights)
    far_ints = far(jnp.concatenate([own_offsets.reshape(-1), slot]))
    far_offsets = far_ints[: 2 * p_dev].reshape(2, p_dev)
    far_slot = far_ints[2 * p_dev :]
    for section in range(last):
        partner = from_partner(image, "sub", section)
        mine = merge_matrix(offsets[section, 0, 0], weights[section, 0, 0])
        theirs = merge_matrix(offsets[section, 0, 1], weights[section, 0, 1])
        merged = jnp.dot(mine, image, preferred_element_type=jnp.float32)
        if section == 1:
            labels, merged = lax.optimization_barrier((labels, merged))
            marks = lax.all_to_all(labels, ("sub", "rng"), split_axis=0, concat_axis=0, tiled=True)
        merged = merged + jnp.dot(theirs, partner, preferred_element_type=jnp.float32)
        image = merged.astype(jnp.bfloat16)
        if section == 1:
            marks, image = lax.optimization_barrier((marks, image))
    slots = jnp.arange(devices * capacity, dtype=jnp.int32)[:, None]
    picks = {0: slots == slot[None, :], bit: slots == far_slot[None, :]}
    half = r_dev // 2
    keep_bit = (me_sub >> last) & 1
    kept = lax.dynamic_slice_in_dim(image, keep_bit * half, half, axis=1)
    sent = lax.dynamic_slice_in_dim(image, (1 - keep_bit) * half, half, axis=1)
    old = {0: kept, bit: far(sent)}
    bands = {
        0: (own_offsets, own_weights),
        bit: (far_offsets, far_weights),
    }
    sends = []
    for m in (0, bit):
        starts, kernel = bands[m]
        mine = merge_matrix(starts[0], kernel[0])
        theirs = merge_matrix(starts[1], kernel[1])
        merged = jnp.dot(mine, old[m], preferred_element_type=jnp.float32)
        merged = merged + jnp.dot(theirs, old[m ^ bit], preferred_element_type=jnp.float32)
        piece = merged.astype(jnp.bfloat16)
        rows = piece.reshape(2, p_dev, half).transpose(1, 0, 2).reshape(p_dev, 2 * half)
        send = jnp.dot(picks[m].astype(jnp.bfloat16), rows, preferred_element_type=jnp.float32)
        sends.append(send.astype(jnp.bfloat16).reshape(devices, capacity, 2 * half))
    grid = marks.reshape(n_sub, n_rng * capacity)
    swapped = jnp.stack([grid[s ^ bit] for s in range(n_sub)], axis=0)
    marks = jnp.stack(
        [grid.reshape(devices, capacity), swapped.reshape(devices, capacity)], axis=1
    ).reshape(devices, 2 * capacity)
    payload = jnp.concatenate(sends, axis=1)
    got = lax.all_to_all(payload, ("sub", "rng"), split_axis=0, concat_axis=0, tiled=True)
    span = devices // 2
    tiles = []
    for h in range(2):
        sources = [s for s in range(n_sub) if (s >> last) & 1 == h]
        block_data = jnp.concatenate(
            [got[s * n_rng : (s + 1) * n_rng] for s in sources], axis=0
        ).reshape(span * 2 * capacity, 2 * half)
        block_mark = jnp.concatenate(
            [marks[s * n_rng : (s + 1) * n_rng] for s in sources], axis=0
        ).reshape(span * 2 * capacity)
        place = (jnp.arange(p_dev, dtype=jnp.int32)[:, None] == block_mark[None, :]).astype(jnp.bfloat16)
        tile = jnp.dot(place, block_data, preferred_element_type=jnp.float32).astype(jnp.bfloat16)
        tiles.append(tile.reshape(p_dev, 2, half))
    return jnp.concatenate(tiles, axis=2).transpose(1, 0, 2)


def solution(mesh):
    in_specs = (
        P(None, "sub", "rng"),
        P(),
        P(None, "sub", None, None),
        P(None, "sub", None, None, None, None),
        P("sub", "rng", None, None),
        P("sub", "rng", None),
    )
    out_specs = P(None, "sub", "rng")
    return jax.shard_map(
        on_device, mesh=mesh, in_specs=in_specs, out_specs=out_specs, check_vma=False
    )
```

```python
import jax
import jax.numpy as jnp
from jax import lax
from jax.sharding import PartitionSpec as P

RBLK = 512


def shifted(value, axis, steps):
    count = lax.axis_size(axis)
    first, last = (max(0, -steps), min(count, count - steps))
    return lax.ppermute(value, axis, [(source, source + steps) for source in range(first, last)])


def from_partner(value, axis, apart):
    return lax.ppermute(value, axis, [(i, i ^ 1 << apart) for i in range(lax.axis_size(axis))])


def replica_matrix(chirp, block_len):
    taps_len = chirp.shape[1]
    width = block_len + taps_len
    parts = []
    for part in range(2):
        padded = jnp.concatenate([chirp[part], jnp.zeros((width + 1 - taps_len,), chirp.dtype)])
        tiled = jnp.tile(padded, block_len)[: block_len * width].reshape(block_len, width)
        parts.append(tiled.T)
    h_real, h_imag = (parts[0], parts[1])
    upper = jnp.concatenate([h_real, -h_imag], axis=1)
    lower = jnp.concatenate([h_imag, h_real], axis=1)
    return jnp.concatenate([upper, lower], axis=0)


def merge_matrix(starts, kernel):
    beams = starts.shape[0]
    taps_len = kernel.shape[-1]
    shift = jnp.arange(beams, dtype=jnp.int32)[None, :] - starts[:, None]
    g_real = jnp.zeros((beams, beams), kernel.dtype)
    g_imag = jnp.zeros((beams, beams), kernel.dtype)
    for tap in range(taps_len):
        hit = shift == tap
        g_real = jnp.where(hit, kernel[0][:, tap : tap + 1], g_real)
        g_imag = jnp.where(hit, kernel[1][:, tap : tap + 1], g_imag)
    upper = jnp.concatenate([g_real, -g_imag], axis=1)
    lower = jnp.concatenate([g_imag, g_real], axis=1)
    return jnp.concatenate([upper, lower], axis=0)


def group_slots(dest, devices):
    onehot = (dest[:, None] == jnp.arange(devices, dtype=jnp.int32)[None, :]).astype(jnp.int32)
    return jnp.sum((jnp.cumsum(onehot, axis=0) - 1) * onehot, axis=1)


def on_device(echoes, chirp, offsets, weights, owners, targets):
    p_dev = echoes.shape[1]
    r_dev = echoes.shape[2]
    n_sub = lax.axis_size("sub")
    n_rng = lax.axis_size("rng")
    devices = n_sub * n_rng
    capacity = max(2, 2 * p_dev // devices)
    tail = shifted(echoes, "rng", -1)
    extended = jnp.concatenate([echoes, tail], axis=2)
    matrix = replica_matrix(chirp, RBLK)
    stacked = jnp.concatenate([extended[0], extended[1]], axis=1)
    block_out = jnp.dot(stacked, matrix, preferred_element_type=jnp.float32).astype(jnp.bfloat16)
    pieces = block_out.reshape(p_dev, 2, RBLK)
    image = pieces.transpose(1, 0, 2).reshape(2 * p_dev, r_dev)
    section_count = offsets.shape[0]
    last = section_count - 1
    bit = 1 << last
    me_sub = lax.axis_index("sub")
    far = lambda value: from_partner(value, "sub", last)
    dest = owners.reshape(p_dev)
    aim = targets.reshape(p_dev)
    slot = dest * capacity + group_slots(dest, devices)
    pick = jnp.arange(devices * capacity, dtype=jnp.int32)[:, None] == slot[None, :]
    labels = jnp.sum(jnp.where(pick, aim[None, :] + 1, 0), axis=1).reshape(devices, capacity) - 1
    late = (offsets[last, 0], weights[last, 0], slot)
    late, labels = lax.optimization_barrier((late, labels))
    own_offsets, own_weights, slot = late
    far_weights = far(own_weights)
    far_ints = far(jnp.concatenate([own_offsets.reshape(-1), slot]))
    far_offsets = far_ints[: 2 * p_dev].reshape(2, p_dev)
    far_slot = far_ints[2 * p_dev :]
    for section in range(last):
        partner = from_partner(image, "sub", section)
        mine = merge_matrix(offsets[section, 0, 0], weights[section, 0, 0])
        theirs = merge_matrix(offsets[section, 0, 1], weights[section, 0, 1])
        merged = jnp.dot(mine, image, preferred_element_type=jnp.float32)
        if section == 1:
            labels, merged = lax.optimization_barrier((labels, merged))
            marks = lax.all_to_all(labels, ("sub", "rng"), split_axis=0, concat_axis=0, tiled=True)
        merged = merged + jnp.dot(theirs, partner, preferred_element_type=jnp.float32)
        image = merged.astype(jnp.bfloat16)
        if section == 1:
            marks, image = lax.optimization_barrier((marks, image))
    slots = jnp.arange(devices * capacity, dtype=jnp.int32)[:, None]
    picks = {0: slots == slot[None, :], bit: slots == far_slot[None, :]}
    half = r_dev // 2
    keep_bit = (me_sub >> last) & 1
    kept = lax.dynamic_slice_in_dim(image, keep_bit * half, half, axis=1)
    sent = lax.dynamic_slice_in_dim(image, (1 - keep_bit) * half, half, axis=1)
    old = {0: kept, bit: far(sent)}
    bands = {
        0: (own_offsets, own_weights),
        bit: (far_offsets, far_weights),
    }
    sends = []
    for m in (0, bit):
        starts, kernel = bands[m]
        mine = merge_matrix(starts[0], kernel[0])
        theirs = merge_matrix(starts[1], kernel[1])
        merged = jnp.dot(mine, old[m], preferred_element_type=jnp.float32)
        merged = merged + jnp.dot(theirs, old[m ^ bit], preferred_element_type=jnp.float32)
        piece = merged.astype(jnp.bfloat16)
        rows = piece.reshape(2, p_dev, half).transpose(1, 0, 2).reshape(p_dev, 2 * half)
        send = jnp.dot(picks[m].astype(jnp.bfloat16), rows, preferred_element_type=jnp.float32)
        sends.append(send.astype(jnp.bfloat16).reshape(devices, capacity, 2 * half))
    grid = marks.reshape(n_sub, n_rng * capacity)
    swapped = jnp.stack([grid[s ^ bit] for s in range(n_sub)], axis=0)
    marks = jnp.stack(
        [grid.reshape(devices, capacity), swapped.reshape(devices, capacity)], axis=1
    ).reshape(devices, 2 * capacity)
    payload = jnp.concatenate(sends, axis=1)
    got = lax.all_to_all(payload, ("sub", "rng"), split_axis=0, concat_axis=0, tiled=True)
    span = devices // 2
    tiles = []
    for h in range(2):
        sources = [s for s in range(n_sub) if (s >> last) & 1 == h]
        block_data = jnp.concatenate(
            [got[s * n_rng : (s + 1) * n_rng] for s in sources], axis=0
        ).reshape(span * 2 * capacity, 2 * half)
        block_mark = jnp.concatenate(
            [marks[s * n_rng : (s + 1) * n_rng] for s in sources], axis=0
        ).reshape(span * 2 * capacity)
        place = (jnp.arange(p_dev, dtype=jnp.int32)[:, None] == block_mark[None, :]).astype(jnp.bfloat16)
        tile = jnp.dot(place, block_data, preferred_element_type=jnp.float32).astype(jnp.bfloat16)
        tiles.append(tile.reshape(p_dev, 2, half))
    return jnp.concatenate(tiles, axis=2).transpose(1, 0, 2)


def solution(mesh):
    in_specs = (
        P(None, "sub", "rng"),
        P(),
        P(None, "sub", None, None),
        P(None, "sub", None, None, None, None),
        P("sub", "rng", None, None),
        P("sub", "rng", None),
    )
    out_specs = P(None, "sub", "rng")
    return jax.shard_map(
        on_device, mesh=mesh, in_specs=in_specs, out_specs=out_specs, check_vma=False
    )
```

```python
import jax
import jax.numpy as jnp
from jax import lax
from jax.sharding import PartitionSpec as P

RBLK = 512


def shifted(value, axis, steps):
    count = lax.axis_size(axis)
    first, last = (max(0, -steps), min(count, count - steps))
    return lax.ppermute(value, axis, [(source, source + steps) for source in range(first, last)])


def from_partner(value, axis, apart):
    return lax.ppermute(value, axis, [(i, i ^ 1 << apart) for i in range(lax.axis_size(axis))])


def replica_matrix(chirp, block_len):
    taps_len = chirp.shape[1]
    width = block_len + taps_len
    parts = []
    for part in range(2):
        padded = jnp.concatenate([chirp[part], jnp.zeros((width + 1 - taps_len,), chirp.dtype)])
        tiled = jnp.tile(padded, block_len)[: block_len * width].reshape(block_len, width)
        parts.append(tiled.T)
    h_real, h_imag = (parts[0], parts[1])
    upper = jnp.concatenate([h_real, -h_imag], axis=1)
    lower = jnp.concatenate([h_imag, h_real], axis=1)
    return jnp.concatenate([upper, lower], axis=0)


def merge_matrix(starts, kernel):
    beams = starts.shape[0]
    taps_len = kernel.shape[-1]
    shift = jnp.arange(beams, dtype=jnp.int32)[None, :] - starts[:, None]
    g_real = jnp.zeros((beams, beams), kernel.dtype)
    g_imag = jnp.zeros((beams, beams), kernel.dtype)
    for tap in range(taps_len):
        hit = shift == tap
        g_real = jnp.where(hit, kernel[0][:, tap : tap + 1], g_real)
        g_imag = jnp.where(hit, kernel[1][:, tap : tap + 1], g_imag)
    upper = jnp.concatenate([g_real, -g_imag], axis=1)
    lower = jnp.concatenate([g_imag, g_real], axis=1)
    return jnp.concatenate([upper, lower], axis=0)


def group_slots(dest, devices):
    onehot = (dest[:, None] == jnp.arange(devices, dtype=jnp.int32)[None, :]).astype(jnp.int32)
    return jnp.sum((jnp.cumsum(onehot, axis=0) - 1) * onehot, axis=1)


def on_device(echoes, chirp, offsets, weights, owners, targets):
    p_dev = echoes.shape[1]
    r_dev = echoes.shape[2]
    n_sub = lax.axis_size("sub")
    n_rng = lax.axis_size("rng")
    devices = n_sub * n_rng
    capacity = max(2, 2 * p_dev // devices)
    tail = shifted(echoes, "rng", -1)
    extended = jnp.concatenate([echoes, tail], axis=2)
    matrix = replica_matrix(chirp, RBLK)
    stacked = jnp.concatenate([extended[0], extended[1]], axis=1)
    block_out = jnp.dot(stacked, matrix, preferred_element_type=jnp.float32).astype(jnp.bfloat16)
    pieces = block_out.reshape(p_dev, 2, RBLK)
    image = pieces.transpose(1, 0, 2).reshape(2 * p_dev, r_dev)
    section_count = offsets.shape[0]
    last = section_count - 1
    bit = 1 << last
    me_sub = lax.axis_index("sub")
    far = lambda value: from_partner(value, "sub", last)
    dest = owners.reshape(p_dev)
    aim = targets.reshape(p_dev)
    slot = dest * capacity + group_slots(dest, devices)
    pick = jnp.arange(devices * capacity, dtype=jnp.int32)[:, None] == slot[None, :]
    labels = jnp.sum(jnp.where(pick, aim[None, :] + 1, 0), axis=1).reshape(devices, capacity) - 1
    late = (offsets[last, 0], weights[last, 0], slot)
    late, labels = lax.optimization_barrier((late, labels))
    own_offsets, own_weights, slot = late
    far_weights = far(own_weights)
    far_ints = far(jnp.concatenate([own_offsets.reshape(-1), slot]))
    far_offsets = far_ints[: 2 * p_dev].reshape(2, p_dev)
    far_slot = far_ints[2 * p_dev :]
    for section in range(last):
        partner = from_partner(image, "sub", section)
        band_in = (offsets[section, 0], weights[section, 0])
        if section == 1:
            (band_in, own_offsets, own_weights), image = lax.optimization_barrier(
                ((band_in, own_offsets, own_weights), image)
            )
        mine = merge_matrix(band_in[0][0], band_in[1][0])
        theirs = merge_matrix(band_in[0][1], band_in[1][1])
        merged = jnp.dot(mine, image, preferred_element_type=jnp.float32)
        if section == 1:
            labels, merged = lax.optimization_barrier((labels, merged))
            marks = lax.all_to_all(labels, ("sub", "rng"), split_axis=0, concat_axis=0, tiled=True)
        merged = merged + jnp.dot(theirs, partner, preferred_element_type=jnp.float32)
        image = merged.astype(jnp.bfloat16)
        if section == 1:
            (marks, far_offsets, far_weights), image = lax.optimization_barrier(
                ((marks, far_offsets, far_weights), image)
            )
    slots = jnp.arange(devices * capacity, dtype=jnp.int32)[:, None]
    picks = {0: slots == slot[None, :], bit: slots == far_slot[None, :]}
    half = r_dev // 2
    keep_bit = (me_sub >> last) & 1
    kept = lax.dynamic_slice_in_dim(image, keep_bit * half, half, axis=1)
    sent = lax.dynamic_slice_in_dim(image, (1 - keep_bit) * half, half, axis=1)
    old = {0: kept, bit: far(sent)}
    bands = {
        0: (own_offsets, own_weights),
        bit: (far_offsets, far_weights),
    }
    sends = []
    for m in (0, bit):
        starts, kernel = bands[m]
        mine = merge_matrix(starts[0], kernel[0])
        theirs = merge_matrix(starts[1], kernel[1])
        merged = jnp.dot(mine, old[m], preferred_element_type=jnp.float32)
        merged = merged + jnp.dot(theirs, old[m ^ bit], preferred_element_type=jnp.float32)
        piece = merged.astype(jnp.bfloat16)
        rows = piece.reshape(2, p_dev, half).transpose(1, 0, 2).reshape(p_dev, 2 * half)
        send = jnp.dot(picks[m].astype(jnp.bfloat16), rows, preferred_element_type=jnp.float32)
        sends.append(send.astype(jnp.bfloat16).reshape(devices, capacity, 2 * half))
    grid = marks.reshape(n_sub, n_rng * capacity)
    swapped = jnp.stack([grid[s ^ bit] for s in range(n_sub)], axis=0)
    marks = jnp.stack(
        [grid.reshape(devices, capacity), swapped.reshape(devices, capacity)], axis=1
    ).reshape(devices, 2 * capacity)
    payload = jnp.concatenate(sends, axis=1)
    got = lax.all_to_all(payload, ("sub", "rng"), split_axis=0, concat_axis=0, tiled=True)
    span = devices // 2
    tiles = []
    for h in range(2):
        sources = [s for s in range(n_sub) if (s >> last) & 1 == h]
        block_data = jnp.concatenate(
            [got[s * n_rng : (s + 1) * n_rng] for s in sources], axis=0
        ).reshape(span * 2 * capacity, 2 * half)
        block_mark = jnp.concatenate(
            [marks[s * n_rng : (s + 1) * n_rng] for s in sources], axis=0
        ).reshape(span * 2 * capacity)
        place = (jnp.arange(p_dev, dtype=jnp.int32)[:, None] == block_mark[None, :]).astype(jnp.bfloat16)
        tile = jnp.dot(place, block_data, preferred_element_type=jnp.float32).astype(jnp.bfloat16)
        tiles.append(tile.reshape(p_dev, 2, half))
    return jnp.concatenate(tiles, axis=2).transpose(1, 0, 2)


def solution(mesh):
    in_specs = (
        P(None, "sub", "rng"),
        P(),
        P(None, "sub", None, None),
        P(None, "sub", None, None, None, None),
        P("sub", "rng", None, None),
        P("sub", "rng", None),
    )
    out_specs = P(None, "sub", "rng")
    return jax.shard_map(
        on_device, mesh=mesh, in_specs=in_specs, out_specs=out_specs, check_vma=False
    )
```

```python
import jax
import jax.numpy as jnp
from jax import lax
from jax.sharding import PartitionSpec as P

RBLK = 512


def shifted(value, axis, steps):
    count = lax.axis_size(axis)
    first, last = (max(0, -steps), min(count, count - steps))
    return lax.ppermute(value, axis, [(source, source + steps) for source in range(first, last)])


def from_partner(value, axis, apart):
    return lax.ppermute(value, axis, [(i, i ^ 1 << apart) for i in range(lax.axis_size(axis))])


def replica_matrix(chirp, block_len):
    taps_len = chirp.shape[1]
    width = block_len + taps_len
    parts = []
    for part in range(2):
        padded = jnp.concatenate([chirp[part], jnp.zeros((width + 1 - taps_len,), chirp.dtype)])
        tiled = jnp.tile(padded, block_len)[: block_len * width].reshape(block_len, width)
        parts.append(tiled.T)
    h_real, h_imag = (parts[0], parts[1])
    upper = jnp.concatenate([h_real, -h_imag], axis=1)
    lower = jnp.concatenate([h_imag, h_real], axis=1)
    return jnp.concatenate([upper, lower], axis=0)


def merge_matrix(starts, kernel):
    beams = starts.shape[0]
    taps_len = kernel.shape[-1]
    shift = jnp.arange(beams, dtype=jnp.int32)[None, :] - starts[:, None]
    g_real = jnp.zeros((beams, beams), kernel.dtype)
    g_imag = jnp.zeros((beams, beams), kernel.dtype)
    for tap in range(taps_len):
        hit = shift == tap
        g_real = jnp.where(hit, kernel[0][:, tap : tap + 1], g_real)
        g_imag = jnp.where(hit, kernel[1][:, tap : tap + 1], g_imag)
    upper = jnp.concatenate([g_real, -g_imag], axis=1)
    lower = jnp.concatenate([g_imag, g_real], axis=1)
    return jnp.concatenate([upper, lower], axis=0)


def group_slots(dest, devices):
    onehot = (dest[:, None] == jnp.arange(devices, dtype=jnp.int32)[None, :]).astype(jnp.int32)
    return jnp.sum((jnp.cumsum(onehot, axis=0) - 1) * onehot, axis=1)


def on_device(echoes, chirp, offsets, weights, owners, targets):
    p_dev = echoes.shape[1]
    r_dev = echoes.shape[2]
    n_sub = lax.axis_size("sub")
    n_rng = lax.axis_size("rng")
    devices = n_sub * n_rng
    capacity = max(2, 2 * p_dev // devices)
    tail = shifted(echoes, "rng", -1)
    matrix = replica_matrix(chirp, RBLK)
    span = matrix.shape[0] // 2
    m_local = jnp.concatenate([matrix[:r_dev], matrix[span : span + r_dev]], axis=0)
    m_tail = jnp.concatenate([matrix[r_dev:span], matrix[span + r_dev :]], axis=0)
    local = jnp.dot(
        jnp.concatenate([echoes[0], echoes[1]], axis=1), m_local, preferred_element_type=jnp.float32
    )
    far_part = jnp.dot(
        jnp.concatenate([tail[0], tail[1]], axis=1), m_tail, preferred_element_type=jnp.float32
    )
    block_out = (local + far_part).astype(jnp.bfloat16)
    pieces = block_out.reshape(p_dev, 2, RBLK)
    image = pieces.transpose(1, 0, 2).reshape(2 * p_dev, r_dev)
    section_count = offsets.shape[0]
    last = section_count - 1
    bit = 1 << last
    me_sub = lax.axis_index("sub")
    far = lambda value: from_partner(value, "sub", last)
    dest = owners.reshape(p_dev)
    aim = targets.reshape(p_dev)
    slot = dest * capacity + group_slots(dest, devices)
    pick = jnp.arange(devices * capacity, dtype=jnp.int32)[:, None] == slot[None, :]
    labels = jnp.sum(jnp.where(pick, aim[None, :] + 1, 0), axis=1).reshape(devices, capacity) - 1
    late = (offsets[last, 0], weights[last, 0], slot)
    for section in range(last):
        partner = from_partner(image, "sub", section)
        mine = merge_matrix(offsets[section, 0, 0], weights[section, 0, 0])
        theirs = merge_matrix(offsets[section, 0, 1], weights[section, 0, 1])
        merged = jnp.dot(mine, image, preferred_element_type=jnp.float32)
        if section == 1:
            late, merged = lax.optimization_barrier((late, merged))
            own_offsets, own_weights, slot = late
            far_weights = far(own_weights)
            far_ints = far(jnp.concatenate([own_offsets.reshape(-1), slot]))
            far_offsets = far_ints[: 2 * p_dev].reshape(2, p_dev)
            far_slot = far_ints[2 * p_dev :]
        merged = merged + jnp.dot(theirs, partner, preferred_element_type=jnp.float32)
        image = merged.astype(jnp.bfloat16)
    slots = jnp.arange(devices * capacity, dtype=jnp.int32)[:, None]
    picks = {0: slots == slot[None, :], bit: slots == far_slot[None, :]}
    half = r_dev // 2
    keep_bit = (me_sub >> last) & 1
    kept = lax.dynamic_slice_in_dim(image, keep_bit * half, half, axis=1)
    sent = lax.dynamic_slice_in_dim(image, (1 - keep_bit) * half, half, axis=1)
    old = {0: kept, bit: far(sent)}
    bands = {
        0: (own_offsets, own_weights),
        bit: (far_offsets, far_weights),
    }
    sends = []
    for m in (0, bit):
        starts, kernel = bands[m]
        mine = merge_matrix(starts[0], kernel[0])
        theirs = merge_matrix(starts[1], kernel[1])
        merged = jnp.dot(mine, old[m], preferred_element_type=jnp.float32)
        if m == 0:
            labels, merged = lax.optimization_barrier((labels, merged))
            marks = lax.all_to_all(labels, ("sub", "rng"), split_axis=0, concat_axis=0, tiled=True)
        merged = merged + jnp.dot(theirs, old[m ^ bit], preferred_element_type=jnp.float32)
        piece = merged.astype(jnp.bfloat16)
        rows = piece.reshape(2, p_dev, half).transpose(1, 0, 2).reshape(p_dev, 2 * half)
        send = jnp.dot(picks[m].astype(jnp.bfloat16), rows, preferred_element_type=jnp.float32)
        sends.append(send.astype(jnp.bfloat16).reshape(devices, capacity, 2 * half))
    grid = marks.reshape(n_sub, n_rng * capacity)
    swapped = jnp.stack([grid[s ^ bit] for s in range(n_sub)], axis=0)
    marks = jnp.stack(
        [grid.reshape(devices, capacity), swapped.reshape(devices, capacity)], axis=1
    ).reshape(devices, 2 * capacity)
    payload = jnp.concatenate(sends, axis=1)
    got = lax.all_to_all(payload, ("sub", "rng"), split_axis=0, concat_axis=0, tiled=True)
    span = devices // 2
    tiles = []
    for h in range(2):
        sources = [s for s in range(n_sub) if (s >> last) & 1 == h]
        block_data = jnp.concatenate(
            [got[s * n_rng : (s + 1) * n_rng] for s in sources], axis=0
        ).reshape(span * 2 * capacity, 2 * half)
        block_mark = jnp.concatenate(
            [marks[s * n_rng : (s + 1) * n_rng] for s in sources], axis=0
        ).reshape(span * 2 * capacity)
        place = (jnp.arange(p_dev, dtype=jnp.int32)[:, None] == block_mark[None, :]).astype(jnp.bfloat16)
        tile = jnp.dot(place, block_data, preferred_element_type=jnp.float32).astype(jnp.bfloat16)
        tiles.append(tile.reshape(p_dev, 2, half))
    return jnp.concatenate(tiles, axis=2).transpose(1, 0, 2)


def solution(mesh):
    in_specs = (
        P(None, "sub", "rng"),
        P(),
        P(None, "sub", None, None),
        P(None, "sub", None, None, None, None),
        P("sub", "rng", None, None),
        P("sub", "rng", None),
    )
    out_specs = P(None, "sub", "rng")
    return jax.shard_map(
        on_device, mesh=mesh, in_specs=in_specs, out_specs=out_specs, check_vma=False
    )
```

```python
import jax
import jax.numpy as jnp
from jax import lax
from jax.sharding import PartitionSpec as P

RBLK = 512


def shifted(value, axis, steps):
    count = lax.axis_size(axis)
    first, last = (max(0, -steps), min(count, count - steps))
    return lax.ppermute(value, axis, [(source, source + steps) for source in range(first, last)])


def from_partner(value, axis, apart):
    return lax.ppermute(value, axis, [(i, i ^ 1 << apart) for i in range(lax.axis_size(axis))])


def replica_matrix(chirp, block_len):
    taps_len = chirp.shape[1]
    width = block_len + taps_len
    parts = []
    for part in range(2):
        padded = jnp.concatenate([chirp[part], jnp.zeros((width + 1 - taps_len,), chirp.dtype)])
        tiled = jnp.tile(padded, block_len)[: block_len * width].reshape(block_len, width)
        parts.append(tiled.T)
    h_real, h_imag = (parts[0], parts[1])
    upper = jnp.concatenate([h_real, -h_imag], axis=1)
    lower = jnp.concatenate([h_imag, h_real], axis=1)
    return jnp.concatenate([upper, lower], axis=0)


def merge_matrix(starts, kernel):
    beams = starts.shape[0]
    taps_len = kernel.shape[-1]
    shift = jnp.arange(beams, dtype=jnp.int32)[None, :] - starts[:, None]
    g_real = jnp.zeros((beams, beams), kernel.dtype)
    g_imag = jnp.zeros((beams, beams), kernel.dtype)
    for tap in range(taps_len):
        hit = shift == tap
        g_real = jnp.where(hit, kernel[0][:, tap : tap + 1], g_real)
        g_imag = jnp.where(hit, kernel[1][:, tap : tap + 1], g_imag)
    upper = jnp.concatenate([g_real, -g_imag], axis=1)
    lower = jnp.concatenate([g_imag, g_real], axis=1)
    return jnp.concatenate([upper, lower], axis=0)


def group_slots(dest, devices):
    onehot = (dest[:, None] == jnp.arange(devices, dtype=jnp.int32)[None, :]).astype(jnp.int32)
    return jnp.sum((jnp.cumsum(onehot, axis=0) - 1) * onehot, axis=1)


def on_device(echoes, chirp, offsets, weights, owners, targets):
    p_dev = echoes.shape[1]
    r_dev = echoes.shape[2]
    n_sub = lax.axis_size("sub")
    n_rng = lax.axis_size("rng")
    devices = n_sub * n_rng
    capacity = max(2, 2 * p_dev // devices)
    tail = shifted(echoes, "rng", -1)
    matrix = replica_matrix(chirp, RBLK)
    span = matrix.shape[0] // 2

    def corr(block, start):
        real = jnp.dot(block[0], matrix[start : start + r_dev], preferred_element_type=jnp.float32)
        imag = jnp.dot(
            block[1], matrix[span + start : span + start + r_dev], preferred_element_type=jnp.float32
        )
        return real + imag

    local = corr(echoes, 0)
    block_out = (local + corr(tail, r_dev)).astype(jnp.bfloat16)
    pieces = block_out.reshape(p_dev, 2, RBLK)
    image = pieces.transpose(1, 0, 2).reshape(2 * p_dev, r_dev)
    section_count = offsets.shape[0]
    last = section_count - 1
    bit = 1 << last
    me_sub = lax.axis_index("sub")
    far = lambda value: from_partner(value, "sub", last)
    dest = owners.reshape(p_dev)
    aim = targets.reshape(p_dev)
    slot = dest * capacity + group_slots(dest, devices)
    pick = jnp.arange(devices * capacity, dtype=jnp.int32)[:, None] == slot[None, :]
    labels = jnp.sum(jnp.where(pick, aim[None, :] + 1, 0), axis=1).reshape(devices, capacity) - 1
    late = (offsets[last, 0], weights[last, 0], slot)
    for section in range(last):
        partner = from_partner(image, "sub", section)
        mine = merge_matrix(offsets[section, 0, 0], weights[section, 0, 0])
        theirs = merge_matrix(offsets[section, 0, 1], weights[section, 0, 1])
        merged = jnp.dot(mine, image, preferred_element_type=jnp.float32)
        if section == 1:
            late, merged = lax.optimization_barrier((late, merged))
            own_offsets, own_weights, slot = late
            far_weights = far(own_weights)
            far_ints = far(jnp.concatenate([own_offsets.reshape(-1), slot]))
            far_offsets = far_ints[: 2 * p_dev].reshape(2, p_dev)
            far_slot = far_ints[2 * p_dev :]
        merged = merged + jnp.dot(theirs, partner, preferred_element_type=jnp.float32)
        image = merged.astype(jnp.bfloat16)
    slots = jnp.arange(devices * capacity, dtype=jnp.int32)[:, None]
    picks = {0: slots == slot[None, :], bit: slots == far_slot[None, :]}
    half = r_dev // 2
    keep_bit = (me_sub >> last) & 1
    kept = lax.dynamic_slice_in_dim(image, keep_bit * half, half, axis=1)
    sent = lax.dynamic_slice_in_dim(image, (1 - keep_bit) * half, half, axis=1)
    old = {0: kept, bit: far(sent)}
    bands = {
        0: (own_offsets, own_weights),
        bit: (far_offsets, far_weights),
    }
    sends = []
    for m in (0, bit):
        starts, kernel = bands[m]
        mine = merge_matrix(starts[0], kernel[0])
        theirs = merge_matrix(starts[1], kernel[1])
        merged = jnp.dot(mine, old[m], preferred_element_type=jnp.float32)
        if m == 0:
            labels, merged = lax.optimization_barrier((labels, merged))
            marks = lax.all_to_all(labels, ("sub", "rng"), split_axis=0, concat_axis=0, tiled=True)
        merged = merged + jnp.dot(theirs, old[m ^ bit], preferred_element_type=jnp.float32)
        piece = merged.astype(jnp.bfloat16)
        rows = piece.reshape(2, p_dev, half).transpose(1, 0, 2).reshape(p_dev, 2 * half)
        send = jnp.dot(picks[m].astype(jnp.bfloat16), rows, preferred_element_type=jnp.float32)
        sends.append(send.astype(jnp.bfloat16).reshape(devices, capacity, 2 * half))
    grid = marks.reshape(n_sub, n_rng * capacity)
    swapped = jnp.stack([grid[s ^ bit] for s in range(n_sub)], axis=0)
    marks = jnp.stack(
        [grid.reshape(devices, capacity), swapped.reshape(devices, capacity)], axis=1
    ).reshape(devices, 2 * capacity)
    payload = jnp.concatenate(sends, axis=1)
    got = lax.all_to_all(payload, ("sub", "rng"), split_axis=0, concat_axis=0, tiled=True)
    span = devices // 2
    tiles = []
    for h in range(2):
        sources = [s for s in range(n_sub) if (s >> last) & 1 == h]
        block_data = jnp.concatenate(
            [got[s * n_rng : (s + 1) * n_rng] for s in sources], axis=0
        ).reshape(span * 2 * capacity, 2 * half)
        block_mark = jnp.concatenate(
            [marks[s * n_rng : (s + 1) * n_rng] for s in sources], axis=0
        ).reshape(span * 2 * capacity)
        place = (jnp.arange(p_dev, dtype=jnp.int32)[:, None] == block_mark[None, :]).astype(jnp.bfloat16)
        tile = jnp.dot(place, block_data, preferred_element_type=jnp.float32).astype(jnp.bfloat16)
        tiles.append(tile.reshape(p_dev, 2, half))
    return jnp.concatenate(tiles, axis=2).transpose(1, 0, 2)


def solution(mesh):
    in_specs = (
        P(None, "sub", "rng"),
        P(),
        P(None, "sub", None, None),
        P(None, "sub", None, None, None, None),
        P("sub", "rng", None, None),
        P("sub", "rng", None),
    )
    out_specs = P(None, "sub", "rng")
    return jax.shard_map(
        on_device, mesh=mesh, in_specs=in_specs, out_specs=out_specs, check_vma=False
    )
```

```python
import jax
import jax.numpy as jnp
from jax import lax
from jax.sharding import PartitionSpec as P

RBLK = 512


def shifted(value, axis, steps):
    count = lax.axis_size(axis)
    first, last = (max(0, -steps), min(count, count - steps))
    return lax.ppermute(value, axis, [(source, source + steps) for source in range(first, last)])


def from_partner(value, axis, apart):
    return lax.ppermute(value, axis, [(i, i ^ 1 << apart) for i in range(lax.axis_size(axis))])


def replica_matrix(chirp, block_len):
    taps_len = chirp.shape[1]
    width = block_len + taps_len
    parts = []
    for part in range(2):
        padded = jnp.concatenate([chirp[part], jnp.zeros((width + 1 - taps_len,), chirp.dtype)])
        tiled = jnp.tile(padded, block_len)[: block_len * width].reshape(block_len, width)
        parts.append(tiled.T)
    h_real, h_imag = (parts[0], parts[1])
    upper = jnp.concatenate([h_real, -h_imag], axis=1)
    lower = jnp.concatenate([h_imag, h_real], axis=1)
    return jnp.concatenate([upper, lower], axis=0)


def merge_matrix(starts, kernel):
    beams = starts.shape[0]
    taps_len = kernel.shape[-1]
    shift = jnp.arange(beams, dtype=jnp.int32)[None, :] - starts[:, None]
    g_real = jnp.zeros((beams, beams), kernel.dtype)
    g_imag = jnp.zeros((beams, beams), kernel.dtype)
    for tap in range(taps_len):
        hit = shift == tap
        g_real = jnp.where(hit, kernel[0][:, tap : tap + 1], g_real)
        g_imag = jnp.where(hit, kernel[1][:, tap : tap + 1], g_imag)
    upper = jnp.concatenate([g_real, -g_imag], axis=1)
    lower = jnp.concatenate([g_imag, g_real], axis=1)
    return jnp.concatenate([upper, lower], axis=0)


def group_slots(dest, devices):
    onehot = (dest[:, None] == jnp.arange(devices, dtype=jnp.int32)[None, :]).astype(jnp.int32)
    return jnp.sum((jnp.cumsum(onehot, axis=0) - 1) * onehot, axis=1)


def on_device(echoes, chirp, offsets, weights, owners, targets):
    p_dev = echoes.shape[1]
    r_dev = echoes.shape[2]
    n_sub = lax.axis_size("sub")
    n_rng = lax.axis_size("rng")
    devices = n_sub * n_rng
    capacity = max(2, 2 * p_dev // devices)
    tail = shifted(echoes, "rng", -1)
    matrix = replica_matrix(chirp, RBLK)
    span = matrix.shape[0] // 2
    m_local = jnp.concatenate([matrix[:r_dev], matrix[span : span + r_dev]], axis=0)
    m_tail = jnp.concatenate([matrix[r_dev:span], matrix[span + r_dev :]], axis=0)
    local = jnp.dot(
        jnp.concatenate([echoes[0], echoes[1]], axis=1), m_local, preferred_element_type=jnp.float32
    )
    far_part = jnp.dot(
        jnp.concatenate([tail[0], tail[1]], axis=1), m_tail, preferred_element_type=jnp.float32
    )
    block_out = (local + far_part).astype(jnp.bfloat16)
    pieces = block_out.reshape(p_dev, 2, RBLK)
    image = pieces.transpose(1, 0, 2).reshape(2 * p_dev, r_dev)
    section_count = offsets.shape[0]
    last = section_count - 1
    bit = 1 << last
    me_sub = lax.axis_index("sub")
    far = lambda value: from_partner(value, "sub", last)
    dest = owners.reshape(p_dev)
    aim = targets.reshape(p_dev)
    slot = dest * capacity + group_slots(dest, devices)
    pick = jnp.arange(devices * capacity, dtype=jnp.int32)[:, None] == slot[None, :]
    labels = jnp.sum(jnp.where(pick, aim[None, :] + 1, 0), axis=1).reshape(devices, capacity) - 1
    late = (offsets[last, 0], weights[last, 0], slot)
    for section in range(last):
        partner = from_partner(image, "sub", section)
        mine = merge_matrix(offsets[section, 0, 0], weights[section, 0, 0])
        theirs = merge_matrix(offsets[section, 0, 1], weights[section, 0, 1])
        merged = jnp.dot(mine, image, preferred_element_type=jnp.float32)
        if section == 1:
            late, merged = lax.optimization_barrier((late, merged))
            own_offsets, own_weights, slot = late
            far_weights = far(own_weights)
            far_ints = far(jnp.concatenate([own_offsets.reshape(-1), slot]))
            far_offsets = far_ints[: 2 * p_dev].reshape(2, p_dev)
            far_slot = far_ints[2 * p_dev :]
        merged = merged + jnp.dot(theirs, partner, preferred_element_type=jnp.float32)
        image = merged.astype(jnp.bfloat16)
    slots = jnp.arange(devices * capacity, dtype=jnp.int32)[:, None]
    rows_at = jnp.concatenate(
        [(s // capacity) * (2 * capacity) + i * capacity + s % capacity for i, s in enumerate((slot, far_slot))]
    )
    pick_both = (
        jnp.arange(2 * devices * capacity, dtype=jnp.int32)[:, None] == rows_at[None, :]
    ).astype(jnp.bfloat16)
    half = r_dev // 2
    keep_bit = (me_sub >> last) & 1
    kept = lax.dynamic_slice_in_dim(image, keep_bit * half, half, axis=1)
    sent = lax.dynamic_slice_in_dim(image, (1 - keep_bit) * half, half, axis=1)
    old = {0: kept, bit: far(sent)}
    bands = {
        0: (own_offsets, own_weights),
        bit: (far_offsets, far_weights),
    }
    sends = []
    for m in (0, bit):
        starts, kernel = bands[m]
        mine = merge_matrix(starts[0], kernel[0])
        theirs = merge_matrix(starts[1], kernel[1])
        merged = jnp.dot(mine, old[m], preferred_element_type=jnp.float32)
        if m == 0:
            labels, merged = lax.optimization_barrier((labels, merged))
            marks = lax.all_to_all(labels, ("sub", "rng"), split_axis=0, concat_axis=0, tiled=True)
        merged = merged + jnp.dot(theirs, old[m ^ bit], preferred_element_type=jnp.float32)
        piece = merged.astype(jnp.bfloat16)
        rows = piece.reshape(2, p_dev, half).transpose(1, 0, 2).reshape(p_dev, 2 * half)
        sends.append(rows)
    grid = marks.reshape(n_sub, n_rng * capacity)
    swapped = jnp.stack([grid[s ^ bit] for s in range(n_sub)], axis=0)
    marks = jnp.stack(
        [grid.reshape(devices, capacity), swapped.reshape(devices, capacity)], axis=1
    ).reshape(devices, 2 * capacity)
    payload = jnp.dot(pick_both, jnp.concatenate(sends, axis=0), preferred_element_type=jnp.float32)
    payload = payload.astype(jnp.bfloat16).reshape(devices, 2 * capacity, 2 * half)
    got = lax.all_to_all(payload, ("sub", "rng"), split_axis=0, concat_axis=0, tiled=True)
    span = devices // 2
    tiles = []
    for h in range(2):
        sources = [s for s in range(n_sub) if (s >> last) & 1 == h]
        block_data = jnp.concatenate(
            [got[s * n_rng : (s + 1) * n_rng] for s in sources], axis=0
        ).reshape(span * 2 * capacity, 2 * half)
        block_mark = jnp.concatenate(
            [marks[s * n_rng : (s + 1) * n_rng] for s in sources], axis=0
        ).reshape(span * 2 * capacity)
        place = (jnp.arange(p_dev, dtype=jnp.int32)[:, None] == block_mark[None, :]).astype(jnp.bfloat16)
        tile = jnp.dot(place, block_data, preferred_element_type=jnp.float32).astype(jnp.bfloat16)
        tiles.append(tile.reshape(p_dev, 2, half))
    return jnp.concatenate(tiles, axis=2).transpose(1, 0, 2)


def solution(mesh):
    in_specs = (
        P(None, "sub", "rng"),
        P(),
        P(None, "sub", None, None),
        P(None, "sub", None, None, None, None),
        P("sub", "rng", None, None),
        P("sub", "rng", None),
    )
    out_specs = P(None, "sub", "rng")
    return jax.shard_map(
        on_device, mesh=mesh, in_specs=in_specs, out_specs=out_specs, check_vma=False
    )
```

```python
import jax
import jax.numpy as jnp
from jax import lax
from jax.sharding import PartitionSpec as P

RBLK = 512


def shifted(value, axis, steps):
    count = lax.axis_size(axis)
    first, last = (max(0, -steps), min(count, count - steps))
    return lax.ppermute(value, axis, [(source, source + steps) for source in range(first, last)])


def from_partner(value, axis, apart):
    return lax.ppermute(value, axis, [(i, i ^ 1 << apart) for i in range(lax.axis_size(axis))])


def replica_matrix(chirp, block_len):
    taps_len = chirp.shape[1]
    width = block_len + taps_len
    parts = []
    for part in range(2):
        padded = jnp.concatenate([chirp[part], jnp.zeros((width + 1 - taps_len,), chirp.dtype)])
        tiled = jnp.tile(padded, block_len)[: block_len * width].reshape(block_len, width)
        parts.append(tiled.T)
    h_real, h_imag = (parts[0], parts[1])
    upper = jnp.concatenate([h_real, -h_imag], axis=1)
    lower = jnp.concatenate([h_imag, h_real], axis=1)
    return jnp.concatenate([upper, lower], axis=0)


def merge_matrix(starts, kernel):
    beams = starts.shape[0]
    taps_len = kernel.shape[-1]
    shift = jnp.arange(beams, dtype=jnp.int32)[None, :] - starts[:, None]
    g_real = jnp.zeros((beams, beams), kernel.dtype)
    g_imag = jnp.zeros((beams, beams), kernel.dtype)
    for tap in range(taps_len):
        hit = shift == tap
        g_real = jnp.where(hit, kernel[0][:, tap : tap + 1], g_real)
        g_imag = jnp.where(hit, kernel[1][:, tap : tap + 1], g_imag)
    upper = jnp.concatenate([g_real, -g_imag], axis=1)
    lower = jnp.concatenate([g_imag, g_real], axis=1)
    return jnp.concatenate([upper, lower], axis=0)


def group_slots(dest, devices):
    onehot = (dest[:, None] == jnp.arange(devices, dtype=jnp.int32)[None, :]).astype(jnp.int32)
    return jnp.sum((jnp.cumsum(onehot, axis=0) - 1) * onehot, axis=1)


def on_device(echoes, chirp, offsets, weights, owners, targets):
    p_dev = echoes.shape[1]
    r_dev = echoes.shape[2]
    n_sub = lax.axis_size("sub")
    n_rng = lax.axis_size("rng")
    devices = n_sub * n_rng
    capacity = max(2, 2 * p_dev // devices)
    tail = shifted(echoes, "rng", -1)
    matrix = replica_matrix(chirp, RBLK)
    span = matrix.shape[0] // 2
    m_local = jnp.concatenate([matrix[:r_dev], matrix[span : span + r_dev]], axis=0)
    m_tail = jnp.concatenate([matrix[r_dev:span], matrix[span + r_dev :]], axis=0)
    local = jnp.dot(
        jnp.concatenate([echoes[0], echoes[1]], axis=1), m_local, preferred_element_type=jnp.float32
    )
    far_part = jnp.dot(
        jnp.concatenate([tail[0], tail[1]], axis=1), m_tail, preferred_element_type=jnp.float32
    )
    block_out = (local + far_part).astype(jnp.bfloat16)
    pieces = block_out.reshape(p_dev, 2, RBLK)
    image = pieces.transpose(1, 0, 2).reshape(2 * p_dev, r_dev)
    section_count = offsets.shape[0]
    last = section_count - 1
    bit = 1 << last
    me_sub = lax.axis_index("sub")
    far = lambda value: from_partner(value, "sub", last)
    dest = owners.reshape(p_dev)
    aim = targets.reshape(p_dev)
    slot = dest * capacity + group_slots(dest, devices)
    pick = jnp.arange(devices * capacity, dtype=jnp.int32)[:, None] == slot[None, :]
    labels = jnp.sum(jnp.where(pick, aim[None, :] + 1, 0), axis=1).reshape(devices, capacity) - 1
    late = (offsets[last, 0], weights[last, 0], slot)
    for section in range(last):
        partner = from_partner(image, "sub", section)
        mine = merge_matrix(offsets[section, 0, 0], weights[section, 0, 0])
        theirs = merge_matrix(offsets[section, 0, 1], weights[section, 0, 1])
        merged = jnp.dot(mine, image, preferred_element_type=jnp.float32)
        if section == 1:
            (labels, late), merged = lax.optimization_barrier(((labels, late), merged))
            marks = lax.all_to_all(labels, ("sub", "rng"), split_axis=0, concat_axis=0, tiled=True)
            own_offsets, own_weights, slot = late
            far_weights = far(own_weights)
            far_ints = far(jnp.concatenate([own_offsets.reshape(-1), slot]))
            far_offsets = far_ints[: 2 * p_dev].reshape(2, p_dev)
            far_slot = far_ints[2 * p_dev :]
        merged = merged + jnp.dot(theirs, partner, preferred_element_type=jnp.float32)
        image = merged.astype(jnp.bfloat16)
        if section == 1:
            marks, image = lax.optimization_barrier((marks, image))
    slots = jnp.arange(devices * capacity, dtype=jnp.int32)[:, None]
    picks = {0: slots == slot[None, :], bit: slots == far_slot[None, :]}
    half = r_dev // 2
    keep_bit = (me_sub >> last) & 1
    kept = lax.dynamic_slice_in_dim(image, keep_bit * half, half, axis=1)
    sent = lax.dynamic_slice_in_dim(image, (1 - keep_bit) * half, half, axis=1)
    old = {0: kept, bit: far(sent)}
    bands = {
        0: (own_offsets, own_weights),
        bit: (far_offsets, far_weights),
    }
    sends = []
    for m in (0, bit):
        starts, kernel = bands[m]
        mine = merge_matrix(starts[0], kernel[0])
        theirs = merge_matrix(starts[1], kernel[1])
        merged = jnp.dot(mine, old[m], preferred_element_type=jnp.float32)
        merged = merged + jnp.dot(theirs, old[m ^ bit], preferred_element_type=jnp.float32)
        piece = merged.astype(jnp.bfloat16)
        rows = piece.reshape(2, p_dev, half).transpose(1, 0, 2).reshape(p_dev, 2 * half)
        send = jnp.dot(picks[m].astype(jnp.bfloat16), rows, preferred_element_type=jnp.float32)
        sends.append(send.astype(jnp.bfloat16).reshape(devices, capacity, 2 * half))
    grid = marks.reshape(n_sub, n_rng * capacity)
    swapped = jnp.stack([grid[s ^ bit] for s in range(n_sub)], axis=0)
    marks = jnp.stack(
        [grid.reshape(devices, capacity), swapped.reshape(devices, capacity)], axis=1
    ).reshape(devices, 2 * capacity)
    payload = jnp.concatenate(sends, axis=1)
    got = lax.all_to_all(payload, ("sub", "rng"), split_axis=0, concat_axis=0, tiled=True)
    span = devices // 2
    tiles = []
    for h in range(2):
        sources = [s for s in range(n_sub) if (s >> last) & 1 == h]
        block_data = jnp.concatenate(
            [got[s * n_rng : (s + 1) * n_rng] for s in sources], axis=0
        ).reshape(span * 2 * capacity, 2 * half)
        block_mark = jnp.concatenate(
            [marks[s * n_rng : (s + 1) * n_rng] for s in sources], axis=0
        ).reshape(span * 2 * capacity)
        place = (jnp.arange(p_dev, dtype=jnp.int32)[:, None] == block_mark[None, :]).astype(jnp.bfloat16)
        tile = jnp.dot(place, block_data, preferred_element_type=jnp.float32).astype(jnp.bfloat16)
        tiles.append(tile.reshape(p_dev, 2, half))
    return jnp.concatenate(tiles, axis=2).transpose(1, 0, 2)


def solution(mesh):
    in_specs = (
        P(None, "sub", "rng"),
        P(),
        P(None, "sub", None, None),
        P(None, "sub", None, None, None, None),
        P("sub", "rng", None, None),
        P("sub", "rng", None),
    )
    out_specs = P(None, "sub", "rng")
    return jax.shard_map(
        on_device, mesh=mesh, in_specs=in_specs, out_specs=out_specs, check_vma=False
    )
```

```python
import jax
import jax.numpy as jnp
from jax import lax
from jax.sharding import PartitionSpec as P

RBLK = 512


def shifted(value, axis, steps):
    count = lax.axis_size(axis)
    first, last = (max(0, -steps), min(count, count - steps))
    return lax.ppermute(value, axis, [(source, source + steps) for source in range(first, last)])


def from_partner(value, axis, apart):
    return lax.ppermute(value, axis, [(i, i ^ 1 << apart) for i in range(lax.axis_size(axis))])


def replica_matrix(chirp, block_len):
    taps_len = chirp.shape[1]
    width = block_len + taps_len
    parts = []
    for part in range(2):
        padded = jnp.concatenate([chirp[part], jnp.zeros((width + 1 - taps_len,), chirp.dtype)])
        tiled = jnp.tile(padded, block_len)[: block_len * width].reshape(block_len, width)
        parts.append(tiled.T)
    h_real, h_imag = (parts[0], parts[1])
    upper = jnp.concatenate([h_real, -h_imag], axis=1)
    lower = jnp.concatenate([h_imag, h_real], axis=1)
    return jnp.concatenate([upper, lower], axis=0)


def merge_matrix(starts, kernel):
    beams = starts.shape[0]
    taps_len = kernel.shape[-1]
    shift = jnp.arange(beams, dtype=jnp.int32)[None, :] - starts[:, None]
    g_real = jnp.zeros((beams, beams), kernel.dtype)
    g_imag = jnp.zeros((beams, beams), kernel.dtype)
    for tap in range(taps_len):
        hit = shift == tap
        g_real = jnp.where(hit, kernel[0][:, tap : tap + 1], g_real)
        g_imag = jnp.where(hit, kernel[1][:, tap : tap + 1], g_imag)
    upper = jnp.concatenate([g_real, -g_imag], axis=1)
    lower = jnp.concatenate([g_imag, g_real], axis=1)
    return jnp.concatenate([upper, lower], axis=0)


def group_slots(dest, devices):
    onehot = (dest[:, None] == jnp.arange(devices, dtype=jnp.int32)[None, :]).astype(jnp.int32)
    return jnp.sum((jnp.cumsum(onehot, axis=0) - 1) * onehot, axis=1)


def on_device(echoes, chirp, offsets, weights, owners, targets):
    p_dev = echoes.shape[1]
    r_dev = echoes.shape[2]
    n_sub = lax.axis_size("sub")
    n_rng = lax.axis_size("rng")
    devices = n_sub * n_rng
    capacity = max(2, 2 * p_dev // devices)
    tail = shifted(echoes, "rng", -1)
    matrix = replica_matrix(chirp, RBLK)
    span = matrix.shape[0] // 2
    m_local = jnp.concatenate([matrix[:r_dev], matrix[span : span + r_dev]], axis=0)
    m_tail = jnp.concatenate([matrix[r_dev:span], matrix[span + r_dev :]], axis=0)
    local = jnp.dot(
        jnp.concatenate([echoes[0], echoes[1]], axis=1), m_local, preferred_element_type=jnp.float32
    )
    far_part = jnp.dot(
        jnp.concatenate([tail[0], tail[1]], axis=1), m_tail, preferred_element_type=jnp.float32
    )
    block_out = (local + far_part).astype(jnp.bfloat16)
    pieces = block_out.reshape(p_dev, 2, RBLK)
    image = pieces.transpose(1, 0, 2).reshape(2 * p_dev, r_dev)
    section_count = offsets.shape[0]
    last = section_count - 1
    bit = 1 << last
    me_sub = lax.axis_index("sub")
    far = lambda value: from_partner(value, "sub", last)
    dest = owners.reshape(p_dev)
    aim = targets.reshape(p_dev)
    slot = dest * capacity + group_slots(dest, devices)
    pick = jnp.arange(devices * capacity, dtype=jnp.int32)[:, None] == slot[None, :]
    labels = jnp.sum(jnp.where(pick, aim[None, :] + 1, 0), axis=1).reshape(devices, capacity) - 1
    late = (offsets[last, 0], weights[last, 0], slot)
    for section in range(last):
        partner = from_partner(image, "sub", section)
        mine = merge_matrix(offsets[section, 0, 0], weights[section, 0, 0])
        theirs = merge_matrix(offsets[section, 0, 1], weights[section, 0, 1])
        merged = jnp.dot(mine, image, preferred_element_type=jnp.float32)
        merged = merged + jnp.dot(theirs, partner, preferred_element_type=jnp.float32)
        image = merged.astype(jnp.bfloat16)
        if section == 0:
            late, image = lax.optimization_barrier((late, image))
            own_offsets, own_weights, slot = late
            far_weights = far(own_weights)
            far_ints = far(jnp.concatenate([own_offsets.reshape(-1), slot]))
            far_offsets = far_ints[: 2 * p_dev].reshape(2, p_dev)
            far_slot = far_ints[2 * p_dev :]
    slots = jnp.arange(devices * capacity, dtype=jnp.int32)[:, None]
    picks = {0: slots == slot[None, :], bit: slots == far_slot[None, :]}
    half = r_dev // 2
    keep_bit = (me_sub >> last) & 1
    kept = lax.dynamic_slice_in_dim(image, keep_bit * half, half, axis=1)
    sent = lax.dynamic_slice_in_dim(image, (1 - keep_bit) * half, half, axis=1)
    old = {0: kept, bit: far(sent)}
    bands = {
        0: (own_offsets, own_weights),
        bit: (far_offsets, far_weights),
    }
    sends = []
    for m in (0, bit):
        starts, kernel = bands[m]
        mine = merge_matrix(starts[0], kernel[0])
        theirs = merge_matrix(starts[1], kernel[1])
        merged = jnp.dot(mine, old[m], preferred_element_type=jnp.float32)
        if m == 0:
            labels, merged = lax.optimization_barrier((labels, merged))
            marks = lax.all_to_all(labels, ("sub", "rng"), split_axis=0, concat_axis=0, tiled=True)
        merged = merged + jnp.dot(theirs, old[m ^ bit], preferred_element_type=jnp.float32)
        piece = merged.astype(jnp.bfloat16)
        rows = piece.reshape(2, p_dev, half).transpose(1, 0, 2).reshape(p_dev, 2 * half)
        send = jnp.dot(picks[m].astype(jnp.bfloat16), rows, preferred_element_type=jnp.float32)
        sends.append(send.astype(jnp.bfloat16).reshape(devices, capacity, 2 * half))
    grid = marks.reshape(n_sub, n_rng * capacity)
    swapped = jnp.stack([grid[s ^ bit] for s in range(n_sub)], axis=0)
    marks = jnp.stack(
        [grid.reshape(devices, capacity), swapped.reshape(devices, capacity)], axis=1
    ).reshape(devices, 2 * capacity)
    payload = jnp.concatenate(sends, axis=1)
    got = lax.all_to_all(payload, ("sub", "rng"), split_axis=0, concat_axis=0, tiled=True)
    span = devices // 2
    tiles = []
    for h in range(2):
        sources = [s for s in range(n_sub) if (s >> last) & 1 == h]
        block_data = jnp.concatenate(
            [got[s * n_rng : (s + 1) * n_rng] for s in sources], axis=0
        ).reshape(span * 2 * capacity, 2 * half)
        block_mark = jnp.concatenate(
            [marks[s * n_rng : (s + 1) * n_rng] for s in sources], axis=0
        ).reshape(span * 2 * capacity)
        place = (jnp.arange(p_dev, dtype=jnp.int32)[:, None] == block_mark[None, :]).astype(jnp.bfloat16)
        tile = jnp.dot(place, block_data, preferred_element_type=jnp.float32).astype(jnp.bfloat16)
        tiles.append(tile.reshape(p_dev, 2, half))
    return jnp.concatenate(tiles, axis=2).transpose(1, 0, 2)


def solution(mesh):
    in_specs = (
        P(None, "sub", "rng"),
        P(),
        P(None, "sub", None, None),
        P(None, "sub", None, None, None, None),
        P("sub", "rng", None, None),
        P("sub", "rng", None),
    )
    out_specs = P(None, "sub", "rng")
    return jax.shard_map(
        on_device, mesh=mesh, in_specs=in_specs, out_specs=out_specs, check_vma=False
    )
```

```python
import jax
import jax.numpy as jnp
from jax import lax
from jax.sharding import PartitionSpec as P

RBLK = 512


def shifted(value, axis, steps):
    count = lax.axis_size(axis)
    first, last = (max(0, -steps), min(count, count - steps))
    return lax.ppermute(value, axis, [(source, source + steps) for source in range(first, last)])


def from_partner(value, axis, apart):
    return lax.ppermute(value, axis, [(i, i ^ 1 << apart) for i in range(lax.axis_size(axis))])


def replica_matrix(chirp, block_len):
    taps_len = chirp.shape[1]
    width = block_len + taps_len
    parts = []
    for part in range(2):
        padded = jnp.concatenate([chirp[part], jnp.zeros((width + 1 - taps_len,), chirp.dtype)])
        tiled = jnp.tile(padded, block_len)[: block_len * width].reshape(block_len, width)
        parts.append(tiled.T)
    h_real, h_imag = (parts[0], parts[1])
    upper = jnp.concatenate([h_real, -h_imag], axis=1)
    lower = jnp.concatenate([h_imag, h_real], axis=1)
    return jnp.concatenate([upper, lower], axis=0)


def merge_matrix(starts, kernel):
    beams = starts.shape[0]
    taps_len = kernel.shape[-1]
    shift = jnp.arange(beams, dtype=jnp.int32)[None, :] - starts[:, None]
    g_real = jnp.zeros((beams, beams), kernel.dtype)
    g_imag = jnp.zeros((beams, beams), kernel.dtype)
    for tap in range(taps_len):
        hit = shift == tap
        g_real = jnp.where(hit, kernel[0][:, tap : tap + 1], g_real)
        g_imag = jnp.where(hit, kernel[1][:, tap : tap + 1], g_imag)
    upper = jnp.concatenate([g_real, -g_imag], axis=1)
    lower = jnp.concatenate([g_imag, g_real], axis=1)
    return jnp.concatenate([upper, lower], axis=0)


def group_slots(dest, devices):
    onehot = (dest[:, None] == jnp.arange(devices, dtype=jnp.int32)[None, :]).astype(jnp.int32)
    return jnp.sum((jnp.cumsum(onehot, axis=0) - 1) * onehot, axis=1)


def on_device(echoes, chirp, offsets, weights, owners, targets):
    p_dev = echoes.shape[1]
    r_dev = echoes.shape[2]
    n_sub = lax.axis_size("sub")
    n_rng = lax.axis_size("rng")
    devices = n_sub * n_rng
    capacity = max(2, 2 * p_dev // devices)
    tail = shifted(echoes, "rng", -1)
    matrix = replica_matrix(chirp, RBLK)
    span = matrix.shape[0] // 2
    m_local = jnp.concatenate([matrix[:r_dev], matrix[span : span + r_dev]], axis=0)
    m_tail = jnp.concatenate([matrix[r_dev:span], matrix[span + r_dev :]], axis=0)
    local = jnp.dot(
        jnp.concatenate([echoes[0], echoes[1]], axis=1), m_local, preferred_element_type=jnp.float32
    )
    far_part = jnp.dot(
        jnp.concatenate([tail[0], tail[1]], axis=1), m_tail, preferred_element_type=jnp.float32
    )
    block_out = (local + far_part).astype(jnp.bfloat16)
    pieces = block_out.reshape(p_dev, 2, RBLK)
    image = pieces.transpose(1, 0, 2).reshape(2 * p_dev, r_dev)
    section_count = offsets.shape[0]
    last = section_count - 1
    bit = 1 << last
    me_sub = lax.axis_index("sub")
    far = lambda value: from_partner(value, "sub", last)
    dest = owners.reshape(p_dev)
    aim = targets.reshape(p_dev)
    slot = dest * capacity + group_slots(dest, devices)
    pick = jnp.arange(devices * capacity, dtype=jnp.int32)[:, None] == slot[None, :]
    labels = jnp.sum(jnp.where(pick, aim[None, :] + 1, 0), axis=1).reshape(devices, capacity) - 1
    late = (offsets[last, 0], weights[last, 0], slot)
    for section in range(last):
        partner = from_partner(image, "sub", section)
        mine = merge_matrix(offsets[section, 0, 0], weights[section, 0, 0])
        theirs = merge_matrix(offsets[section, 0, 1], weights[section, 0, 1])
        merged = jnp.dot(mine, image, preferred_element_type=jnp.float32)
        if section == 1:
            labels, merged = lax.optimization_barrier((labels, merged))
            marks = lax.all_to_all(labels, ("sub", "rng"), split_axis=0, concat_axis=0, tiled=True)
        merged = merged + jnp.dot(theirs, partner, preferred_element_type=jnp.float32)
        image = merged.astype(jnp.bfloat16)
        if section == 1:
            marks, image = lax.optimization_barrier((marks, image))
        if section == 0:
            late, image = lax.optimization_barrier((late, image))
            own_offsets, own_weights, slot = late
            far_weights = far(own_weights)
            far_ints = far(jnp.concatenate([own_offsets.reshape(-1), slot]))
            far_offsets = far_ints[: 2 * p_dev].reshape(2, p_dev)
            far_slot = far_ints[2 * p_dev :]
    slots = jnp.arange(devices * capacity, dtype=jnp.int32)[:, None]
    picks = {0: slots == slot[None, :], bit: slots == far_slot[None, :]}
    half = r_dev // 2
    keep_bit = (me_sub >> last) & 1
    kept = lax.dynamic_slice_in_dim(image, keep_bit * half, half, axis=1)
    sent = lax.dynamic_slice_in_dim(image, (1 - keep_bit) * half, half, axis=1)
    old = {0: kept, bit: far(sent)}
    bands = {
        0: (own_offsets, own_weights),
        bit: (far_offsets, far_weights),
    }
    sends = []
    for m in (0, bit):
        starts, kernel = bands[m]
        mine = merge_matrix(starts[0], kernel[0])
        theirs = merge_matrix(starts[1], kernel[1])
        merged = jnp.dot(mine, old[m], preferred_element_type=jnp.float32)
        merged = merged + jnp.dot(theirs, old[m ^ bit], preferred_element_type=jnp.float32)
        piece = merged.astype(jnp.bfloat16)
        rows = piece.reshape(2, p_dev, half).transpose(1, 0, 2).reshape(p_dev, 2 * half)
        send = jnp.dot(picks[m].astype(jnp.bfloat16), rows, preferred_element_type=jnp.float32)
        sends.append(send.astype(jnp.bfloat16).reshape(devices, capacity, 2 * half))
    grid = marks.reshape(n_sub, n_rng * capacity)
    swapped = jnp.stack([grid[s ^ bit] for s in range(n_sub)], axis=0)
    marks = jnp.stack(
        [grid.reshape(devices, capacity), swapped.reshape(devices, capacity)], axis=1
    ).reshape(devices, 2 * capacity)
    payload = jnp.concatenate(sends, axis=1)
    got = lax.all_to_all(payload, ("sub", "rng"), split_axis=0, concat_axis=0, tiled=True)
    span = devices // 2
    tiles = []
    for h in range(2):
        sources = [s for s in range(n_sub) if (s >> last) & 1 == h]
        block_data = jnp.concatenate(
            [got[s * n_rng : (s + 1) * n_rng] for s in sources], axis=0
        ).reshape(span * 2 * capacity, 2 * half)
        block_mark = jnp.concatenate(
            [marks[s * n_rng : (s + 1) * n_rng] for s in sources], axis=0
        ).reshape(span * 2 * capacity)
        place = (jnp.arange(p_dev, dtype=jnp.int32)[:, None] == block_mark[None, :]).astype(jnp.bfloat16)
        tile = jnp.dot(place, block_data, preferred_element_type=jnp.float32).astype(jnp.bfloat16)
        tiles.append(tile.reshape(p_dev, 2, half))
    return jnp.concatenate(tiles, axis=2).transpose(1, 0, 2)


def solution(mesh):
    in_specs = (
        P(None, "sub", "rng"),
        P(),
        P(None, "sub", None, None),
        P(None, "sub", None, None, None, None),
        P("sub", "rng", None, None),
        P("sub", "rng", None),
    )
    out_specs = P(None, "sub", "rng")
    return jax.shard_map(
        on_device, mesh=mesh, in_specs=in_specs, out_specs=out_specs, check_vma=False
    )
```

```python
import jax
import jax.numpy as jnp
from jax import lax
from jax.sharding import PartitionSpec as P

RBLK = 512


def shifted(value, axis, steps):
    count = lax.axis_size(axis)
    first, last = (max(0, -steps), min(count, count - steps))
    return lax.ppermute(value, axis, [(source, source + steps) for source in range(first, last)])


def from_partner(value, axis, apart):
    return lax.ppermute(value, axis, [(i, i ^ 1 << apart) for i in range(lax.axis_size(axis))])


def replica_matrix(chirp, block_len):
    taps_len = chirp.shape[1]
    width = block_len + taps_len
    parts = []
    for part in range(2):
        padded = jnp.concatenate([chirp[part], jnp.zeros((width + 1 - taps_len,), chirp.dtype)])
        tiled = jnp.tile(padded, block_len)[: block_len * width].reshape(block_len, width)
        parts.append(tiled.T)
    h_real, h_imag = (parts[0], parts[1])
    upper = jnp.concatenate([h_real, -h_imag], axis=1)
    lower = jnp.concatenate([h_imag, h_real], axis=1)
    return jnp.concatenate([upper, lower], axis=0)


def merge_matrix(starts, kernel):
    beams = starts.shape[0]
    taps_len = kernel.shape[-1]
    shift = jnp.arange(beams, dtype=jnp.int32)[None, :] - starts[:, None]
    g_real = jnp.zeros((beams, beams), kernel.dtype)
    g_imag = jnp.zeros((beams, beams), kernel.dtype)
    for tap in range(taps_len):
        hit = shift == tap
        g_real = jnp.where(hit, kernel[0][:, tap : tap + 1], g_real)
        g_imag = jnp.where(hit, kernel[1][:, tap : tap + 1], g_imag)
    upper = jnp.concatenate([g_real, -g_imag], axis=1)
    lower = jnp.concatenate([g_imag, g_real], axis=1)
    return jnp.concatenate([upper, lower], axis=0)


def group_slots(dest, devices):
    onehot = (dest[:, None] == jnp.arange(devices, dtype=jnp.int32)[None, :]).astype(jnp.int32)
    return jnp.sum((jnp.cumsum(onehot, axis=0) - 1) * onehot, axis=1)


def on_device(echoes, chirp, offsets, weights, owners, targets):
    p_dev = echoes.shape[1]
    r_dev = echoes.shape[2]
    n_sub = lax.axis_size("sub")
    n_rng = lax.axis_size("rng")
    devices = n_sub * n_rng
    capacity = max(2, 2 * p_dev // devices)
    tail = shifted(echoes, "rng", -1)
    matrix = replica_matrix(chirp, RBLK)
    span = matrix.shape[0] // 2
    m_local = jnp.concatenate([matrix[:r_dev], matrix[span : span + r_dev]], axis=0)
    m_tail = jnp.concatenate([matrix[r_dev:span], matrix[span + r_dev :]], axis=0)
    local = jnp.dot(
        jnp.concatenate([echoes[0], echoes[1]], axis=1), m_local, preferred_element_type=jnp.float32
    )
    far_part = jnp.dot(
        jnp.concatenate([tail[0], tail[1]], axis=1), m_tail, preferred_element_type=jnp.float32
    )
    block_out = (local + far_part).astype(jnp.bfloat16)
    pieces = block_out.reshape(p_dev, 2, RBLK)
    image = pieces.transpose(1, 0, 2).reshape(2 * p_dev, r_dev)
    section_count = offsets.shape[0]
    last = section_count - 1
    bit = 1 << last
    me_sub = lax.axis_index("sub")
    far = lambda value: from_partner(value, "sub", last)
    dest = owners.reshape(p_dev)
    aim = targets.reshape(p_dev)
    slot = dest * capacity + group_slots(dest, devices)
    pick = jnp.arange(devices * capacity, dtype=jnp.int32)[:, None] == slot[None, :]
    labels = jnp.sum(jnp.where(pick, aim[None, :] + 1, 0), axis=1).reshape(devices, capacity) - 1
    late = (offsets[last, 0], weights[last, 0], slot)
    for section in range(last):
        partner = from_partner(image, "sub", section)
        mine = merge_matrix(offsets[section, 0, 0], weights[section, 0, 0])
        theirs = merge_matrix(offsets[section, 0, 1], weights[section, 0, 1])
        merged = jnp.dot(mine, image, preferred_element_type=jnp.float32)
        merged = merged + jnp.dot(theirs, partner, preferred_element_type=jnp.float32)
        image = merged.astype(jnp.bfloat16)
        if section == 0:
            late, image = lax.optimization_barrier((late, image))
            own_offsets, own_weights, slot = late
            far_weights = far(own_weights)
            far_ints = far(jnp.concatenate([own_offsets.reshape(-1), slot]))
            far_offsets = far_ints[: 2 * p_dev].reshape(2, p_dev)
            far_slot = far_ints[2 * p_dev :]
    slots = jnp.arange(devices * capacity, dtype=jnp.int32)[:, None]
    picks = {0: slots == slot[None, :], bit: slots == far_slot[None, :]}
    half = r_dev // 2
    keep_bit = (me_sub >> last) & 1
    kept = lax.dynamic_slice_in_dim(image, keep_bit * half, half, axis=1)
    sent = lax.dynamic_slice_in_dim(image, (1 - keep_bit) * half, half, axis=1)
    bands = {
        0: (own_offsets, own_weights),
        bit: (far_offsets, far_weights),
    }
    sends = []
    built = {m: tuple(merge_matrix(bands[m][0][i], bands[m][1][i]) for i in range(2)) for m in (0, bit)}
    built, kept = lax.optimization_barrier((built, kept))
    old = {0: kept, bit: far(sent)}
    for m in (0, bit):
        mine, theirs = built[m]
        merged = jnp.dot(mine, old[m], preferred_element_type=jnp.float32)
        if m == 0:
            labels, merged = lax.optimization_barrier((labels, merged))
            marks = lax.all_to_all(labels, ("sub", "rng"), split_axis=0, concat_axis=0, tiled=True)
        merged = merged + jnp.dot(theirs, old[m ^ bit], preferred_element_type=jnp.float32)
        piece = merged.astype(jnp.bfloat16)
        rows = piece.reshape(2, p_dev, half).transpose(1, 0, 2).reshape(p_dev, 2 * half)
        send = jnp.dot(picks[m].astype(jnp.bfloat16), rows, preferred_element_type=jnp.float32)
        sends.append(send.astype(jnp.bfloat16).reshape(devices, capacity, 2 * half))
    grid = marks.reshape(n_sub, n_rng * capacity)
    swapped = jnp.stack([grid[s ^ bit] for s in range(n_sub)], axis=0)
    marks = jnp.stack(
        [grid.reshape(devices, capacity), swapped.reshape(devices, capacity)], axis=1
    ).reshape(devices, 2 * capacity)
    payload = jnp.concatenate(sends, axis=1)
    got = lax.all_to_all(payload, ("sub", "rng"), split_axis=0, concat_axis=0, tiled=True)
    span = devices // 2
    tiles = []
    for h in range(2):
        sources = [s for s in range(n_sub) if (s >> last) & 1 == h]
        block_data = jnp.concatenate(
            [got[s * n_rng : (s + 1) * n_rng] for s in sources], axis=0
        ).reshape(span * 2 * capacity, 2 * half)
        block_mark = jnp.concatenate(
            [marks[s * n_rng : (s + 1) * n_rng] for s in sources], axis=0
        ).reshape(span * 2 * capacity)
        place = (jnp.arange(p_dev, dtype=jnp.int32)[:, None] == block_mark[None, :]).astype(jnp.bfloat16)
        tile = jnp.dot(place, block_data, preferred_element_type=jnp.float32).astype(jnp.bfloat16)
        tiles.append(tile.reshape(p_dev, 2, half))
    return jnp.concatenate(tiles, axis=2).transpose(1, 0, 2)


def solution(mesh):
    in_specs = (
        P(None, "sub", "rng"),
        P(),
        P(None, "sub", None, None),
        P(None, "sub", None, None, None, None),
        P("sub", "rng", None, None),
        P("sub", "rng", None),
    )
    out_specs = P(None, "sub", "rng")
    return jax.shard_map(
        on_device, mesh=mesh, in_specs=in_specs, out_specs=out_specs, check_vma=False
    )
```
